128 devices in a mesh: dp: 16 (over x, y_lo, core), ctx: 8 (over z, y_hi).
Axes of the slice: x: 4, y: 4 (y_hi: 2, y_lo: 2; y = y_hi * 2 + y_lo), z: 4, core: 2. Of those that a mesh axis runs over, the one named last changes fastest.
Arguments:
- ids: int32 [2048], P('ctx'), may hold values from 0 to 511
- tags: int32 [2048], P('ctx'), may hold values from 0 to 3
- embed: bfloat16 [512, 4096], P(None, 'dp'), may hold values from -21 to 21
- gain: float32 [4096], P('dp'), may hold values from 0.5 to 1.5
- w_in: bfloat16 [3, 4096, 4096], P(None, None, 'dp'), may hold values from -0.125 to 0.125
- short_filt: float32 [3, 7, 4096], P(None, None, 'dp'), may hold values from -2.4 to 2.4
- mr_filt: float32 [128, 4096], P(None, 'dp'), may hold values from -0.9 to 0.9
- rates: float32 [4096], P('dp'), may hold values from 0.004 to 0.12
- w_out: bfloat16 [4096, 4096], P('dp'), may hold values from -0.125 to 0.125
- w_tag: bfloat16 [4096, 4], P('dp'), may hold values from -0.25 to 0.25
Outputs:
- loss: float32 [], replicated
- block_out: bfloat16 [2048, 4096], P('ctx', 'dp')
- d_embed: float32 [512, 4096], P('ctx', 'dp')
- d_gain: float32 [4096], P('dp')
- d_w_in: float32 [3, 4096, 4096], P(None, 'ctx', 'dp')
- d_short: float32 [3, 7, 4096], P(None, None, 'dp')
- d_mr: float32 [128, 4096], P(None, 'dp')
- d_rates: float32 [4096], P('dp')
- d_w_out: float32 [4096, 4096], P('dp', 'ctx')
- d_w_tag: float32 [4096, 4], P('dp')
The draws below stay inside these ranges and needn't reach their ends.
All inputs are finite; a program needn't handle non-finite values.
Results may differ from the reference program's by a relative error of at most 0.025.
Values may be sent and summed in bfloat16 or wider, within the bound.
No kernel may reach another device: no remote copies, remote signals or barrier semaphores. Data moves between devices by JAX's collectives and lax.ppermute only.
A program may use at most 128 MiB of HBM per device.

```python
import math
import jax
import jax.numpy as jnp
from jax import lax

D = 4096
VOCAB = 512
TAGS = 4
SHORT = 7
MEDIUM = 128
SEQ = 2048


def draw_embed(key, part):
    key_base, key_rows, key_cols = jax.random.split(key, 3)
    base = jnp.clip(jax.random.normal(key_base, (VOCAB, D), jnp.float32), -4.0, 4.0)
    row_scale = 0.3 * jnp.exp(jax.random.uniform(key_rows, (VOCAB, 1), jnp.float32, 0.0, math.log(10.0)))
    position = jnp.arange(D).astype(jnp.float32)[None, :] / D
    col_scale = 0.4 * jnp.exp(math.log(3.0) * position + 0.35 * jax.random.uniform(key_cols, (1, D), jnp.float32, -1.0, 1.0))
    return (base * row_scale * col_scale).astype(jnp.bfloat16)


def set_ends(entries, rng, smallest, high):
    longest = entries.shape.index(max(entries.shape))
    spots = []
    for shift in (0, 1):
        where = [jax.random.randint(jax.random.fold_in(rng, axis), (), 0, length) for axis, length in enumerate(entries.shape)]
        where[longest] = (where[longest] + shift) % entries.shape[longest]
        spots.append(tuple(where))
    return entries.at[spots[0]].set(smallest).at[spots[1]].set(high)


def strengthened(entries, key, source, target, shards_of, factor):
    owner, partner = [(jnp.arange(entries.shape[dim]) // (entries.shape[dim] // shards_of)).reshape([-1 if axis == dim else 1 for axis in range(entries.ndim)]) for dim in (source, target)]
    chosen = jax.random.permutation(key, shards_of)[partner]
    strong = (owner == chosen) | (owner == (partner + shards_of // 2) % shards_of)
    return jnp.where(strong, factor * entries, entries)


def steps_of(stream_key, dims, pieces, smallest, top_value):
    level = 1.0
    for dim, blocks in pieces:
        draws = jax.random.uniform(jax.random.fold_in(jax.random.fold_in(stream_key, 6), dim), (blocks,), jnp.float32, smallest / len(pieces), top_value / len(pieces))
        level = level * jnp.repeat(jnp.exp(draws), dims[dim] // blocks).reshape((-1,) + (1,) * (len(dims) - 1 - dim))
    return level


def noise(rng, dims, spread, limit, cuts=(), held_as=jnp.bfloat16):
    entries = spread * jax.random.normal(rng, dims, jnp.float32)
    if cuts:
        entries = entries * steps_of(rng, dims, cuts, -0.22, 0.18)
    return jnp.clip(entries, -limit, limit).astype(held_as)


def heavy_noise(key, shape, spread, bound, pieces, heavy, held_as=jnp.bfloat16):
    result = spread * jax.random.normal(key, shape, jnp.float32)
    if pieces:
        result = result * steps_of(key, shape, pieces, -0.22, 0.18)
    return jnp.clip(strengthened(result, jax.random.fold_in(key, 3), *heavy), -bound, bound).astype(held_as)


def setup_inputs(seed: int = 0) -> dict:
    keys = jax.random.split(jax.random.key(seed), 11)
    ids = set_ends(jax.random.randint(keys[0], (SEQ,), 0, VOCAB), jax.random.fold_in(keys[0], 1), 0, VOCAB - 1).astype(jnp.int32)
    tags = set_ends(jax.random.randint(keys[1], (SEQ,), 0, TAGS), jax.random.fold_in(keys[1], 1), 0, TAGS - 1).astype(jnp.int32)
    embed = draw_embed(jax.random.fold_in(keys[10], 71), 0)
    gain = jnp.clip(1.0 + 0.1 * jax.random.normal(keys[3], (D,), jnp.float32), 0.5, 1.5)
    w_in = heavy_noise(keys[4], (3, D, D), D ** -0.5, 0.125, ((2, 16),), (2, 1, 16, 2.0))
    short_filt = noise(keys[5], (3, SHORT, D), 0.4, 2.4, ((2, 16),), jnp.float32)
    mr_filt = noise(keys[6], (MEDIUM, D), 0.15, 0.9, ((1, 16),), jnp.float32)
    rates = jnp.clip(jnp.exp(math.log(0.12) - 3.4011973 * jax.random.uniform(keys[7], (D,), jnp.float32) ** steps_of(keys[7], (D,), ((0, 16),), -0.2, 0.2)), 0.004, 0.12)
    w_out = heavy_noise(keys[8], (D, D), D ** -0.5, 0.125, ((0, 16),), (0, 1, 16, 2.0))
    w_tag = noise(keys[9], (D, TAGS), (D // 9) ** -0.5, 0.25, ((0, 16),))
    return {"ids": ids, "tags": tags, "embed": embed, "gain": gain, "w_in": w_in, "short_filt": short_filt, "mr_filt": mr_filt, "rates": rates, "w_out": w_out, "w_tag": w_tag}


def reference(ids, tags, embed, gain, w_in, short_filt, mr_filt, rates, w_out, w_tag):
    f32 = jnp.float32
    high = lax.Precision.HIGHEST
    x0 = embed[ids]
    xf = x0.astype(f32)
    r = lax.rsqrt(lax.optimization_barrier(jnp.mean(xf * xf, axis=1, keepdims=True)) + 1e-06)
    u = (xf * r * gain[None, :]).astype(jnp.bfloat16)
    proj = jnp.stack([jnp.dot(u, w_in[j], preferred_element_type=f32) for j in range(3)]).astype(jnp.bfloat16)
    pf = proj.astype(f32)
    ppad = jnp.pad(pf, ((0, 0), (SHORT - 1, 0), (0, 0)))
    z = jnp.zeros_like(pf)
    for s in range(SHORT):
        z = z + short_filt[:, s, None, :] * ppad[:, SHORT - 1 - s:SHORT - 1 - s + SEQ, :]
    q, k, v = (z[0], z[1], z[2])
    kv = (k * v).astype(jnp.bfloat16)
    kvf = kv.astype(f32)
    lags = jnp.arange(MEDIUM).astype(f32)[:, None]
    decay = jnp.exp(-rates[None, :] * lags)
    g = mr_filt * decay
    kvpad = jnp.pad(kvf, ((MEDIUM - 1, 0), (0, 0)))

    def conv_step(s, acc):
        start = (MEDIUM - 1 - s).astype(jnp.int32)
        return acc + g[s] * lax.dynamic_slice_in_dim(kvpad, start, SEQ, 0)
    m = lax.fori_loop(jnp.int32(0), jnp.int32(MEDIUM), conv_step, jnp.zeros((SEQ, D), f32))
    h = (q * m).astype(jnp.bfloat16)
    y = jnp.dot(h, w_out, preferred_element_type=f32)
    out = xf + y
    block_out = out.astype(jnp.bfloat16)
    logits = jnp.dot(block_out, w_tag, preferred_element_type=f32)
    top = lax.optimization_barrier(jnp.max(logits, axis=1))
    lse = top + jnp.log(lax.optimization_barrier(jnp.sum(jnp.exp(logits - top[:, None]), axis=1)))
    tag_hot = (tags[:, None] == jnp.arange(TAGS)[None, :]).astype(f32)
    picked = lax.optimization_barrier(jnp.sum(logits * tag_hot, axis=1))
    loss = jnp.sum(lse - picked) / SEQ
    dlog = jnp.exp(logits - lse[:, None]) - tag_hot
    dout = jnp.dot(dlog, w_tag.astype(f32).T, precision=high)
    d_w_tag = jnp.dot(block_out.astype(f32).T, dlog, precision=high)
    dy = dout.astype(jnp.bfloat16)
    dh = jnp.dot(dy, w_out.T, preferred_element_type=f32)
    d_w_out = jnp.dot(h.T, dy, preferred_element_type=f32)
    dq = dh * m
    dm = dh * q
    dmpad = jnp.pad(dm, ((0, MEDIUM - 1), (0, 0)))

    def back_step(s, acc):
        return acc + g[s] * lax.dynamic_slice_in_dim(dmpad, s.astype(jnp.int32), SEQ, 0)
    dkv = lax.fori_loop(jnp.int32(0), jnp.int32(MEDIUM), back_step, jnp.zeros((SEQ, D), f32))

    def corr_lag(s):
        start = (MEDIUM - 1 - s).astype(jnp.int32)
        return lax.optimization_barrier(jnp.sum(dm * lax.dynamic_slice_in_dim(kvpad, start, SEQ, 0), axis=0))
    corr = lax.map(corr_lag, jnp.arange(MEDIUM).astype(jnp.int32))
    d_mr = corr * decay
    d_rates = -lax.optimization_barrier(jnp.sum(lags * mr_filt * d_mr, axis=0))
    dz = jnp.stack([dq, dkv * v, dkv * k])
    dzpad = jnp.pad(dz, ((0, 0), (0, SHORT - 1), (0, 0)))
    dp = jnp.zeros_like(dz)
    shorts = []
    for s in range(SHORT):
        dp = dp + short_filt[:, s, None, :] * dzpad[:, s:s + SEQ, :]
        shorts.append(lax.optimization_barrier(jnp.sum(dz * ppad[:, SHORT - 1 - s:SHORT - 1 - s + SEQ, :], axis=1)))
    d_short = jnp.stack(shorts, axis=1)
    dpb = dp.astype(jnp.bfloat16)
    d_w_in = jnp.stack([jnp.dot(u.T, dpb[j], preferred_element_type=f32) for j in range(3)])
    du = jnp.dot(dpb[0], w_in[0].T, preferred_element_type=f32)
    du = du + jnp.dot(dpb[1], w_in[1].T, preferred_element_type=f32)
    du = du + jnp.dot(dpb[2], w_in[2].T, preferred_element_type=f32)
    d_gain = lax.optimization_barrier(jnp.sum(du * xf * r, axis=0))
    dn = du * gain[None, :]
    row_dot = lax.optimization_barrier(jnp.mean(dn * xf, axis=1, keepdims=True))
    dx0 = dout + r * (dn - xf * r * r * row_dot)
    id_hot = (ids[:, None] == jnp.arange(VOCAB)[None, :]).astype(f32)
    d_embed = jnp.dot(id_hot.T, dx0, precision=high)
    return (loss, block_out, d_embed, d_gain, d_w_in, d_short, d_mr, d_rates, d_w_out, d_w_tag)
```

```python
import jax
import jax.numpy as jnp
from jax import lax
from jax.sharding import PartitionSpec as P
from jax.experimental import pallas as pl
from jax.experimental.pallas import tpu as pltpu

LANES = 128
ROW_BLOCK = 64


def medium_forward(kv_ext, taps_eff, rows):
    span, width = taps_eff.shape

    def kernel(kv_ref, g_ref, m_ref):
        for rb in range(0, rows, ROW_BLOCK):
            acc = jnp.zeros((ROW_BLOCK, LANES), jnp.float32)
            for s in range(span):
                start = span - 1 - s + rb
                acc = acc + g_ref[s : s + 1, :] * kv_ref[start : start + ROW_BLOCK, :]
            m_ref[rb : rb + ROW_BLOCK, :] = acc

    ext = kv_ext.shape[0]
    return pl.pallas_call(
        kernel,
        out_shape=jax.ShapeDtypeStruct((rows, width), jnp.float32),
        grid=(width // LANES,),
        in_specs=[
            pl.BlockSpec((ext, LANES), lambda c: (0, c)),
            pl.BlockSpec((span, LANES), lambda c: (0, c)),
        ],
        out_specs=pl.BlockSpec((rows, LANES), lambda c: (0, c)),
    )(kv_ext, taps_eff)


def medium_backward(dm_ext, kv_ext, taps_eff, rows):
    span, width = taps_eff.shape

    def kernel(dm_ref, kv_ref, g_ref, dkv_ref, corr_ref):
        for rb in range(0, rows, ROW_BLOCK):
            acc = jnp.zeros((ROW_BLOCK, LANES), jnp.float32)
            for s in range(span):
                acc = acc + g_ref[s : s + 1, :] * dm_ref[s + rb : s + rb + ROW_BLOCK, :]
            dkv_ref[rb : rb + ROW_BLOCK, :] = acc
        for s0 in range(0, span, 8):
            parts = []
            for s in range(s0, s0 + 8):
                start = span - 1 - s
                part = jnp.zeros((8, LANES), jnp.float32)
                for rb in range(0, rows, 8):
                    part = part + dm_ref[rb : rb + 8, :] * kv_ref[start + rb : start + rb + 8, :]
                parts.append(jnp.sum(part, axis=0, keepdims=True))
            corr_ref[s0 : s0 + 8, :] = jnp.concatenate(parts, axis=0)

    ext = kv_ext.shape[0]
    return pl.pallas_call(
        kernel,
        out_shape=(
            jax.ShapeDtypeStruct((rows, width), jnp.float32),
            jax.ShapeDtypeStruct((span, width), jnp.float32),
        ),
        grid=(width // LANES,),
        in_specs=[
            pl.BlockSpec((dm_ext.shape[0], LANES), lambda c: (0, c)),
            pl.BlockSpec((ext, LANES), lambda c: (0, c)),
            pl.BlockSpec((span, LANES), lambda c: (0, c)),
        ],
        out_specs=(
            pl.BlockSpec((rows, LANES), lambda c: (0, c)),
            pl.BlockSpec((span, LANES), lambda c: (0, c)),
        ),
    )(dm_ext, kv_ext, taps_eff)


def shifted(block, axis, distance):
    devices = range(lax.axis_size(axis))
    route = [(i - distance, i) for i in devices if i - distance in devices]
    return lax.ppermute(block, axis, route)


def short_filter(padded, filters, count):
    taps = filters.shape[1]
    total = jnp.zeros((count,) + padded.shape[1:], jnp.float32)
    for s in range(taps):
        total = total + filters[None, :, s, :] * padded[taps - 1 - s : taps - 1 - s + count].astype(
            jnp.float32
        )
    return total


def body(ids, tags, embed, gain, w_in, short_filt, mr_filt, rates, w_out, w_tag):
    f32 = jnp.float32
    high = lax.Precision.HIGHEST
    rows = ids.shape[0]
    width = w_in.shape[1]
    taps = short_filt.shape[1]
    span = mr_filt.shape[0]
    n_ctx = lax.axis_size("ctx")
    id_hot = (ids[:, None] == jnp.arange(embed.shape[0])[None, :]).astype(jnp.bfloat16)
    x0 = jnp.dot(id_hot, embed, preferred_element_type=f32)
    row_sq = lax.psum(jnp.sum(x0 * x0, axis=1), "dp")
    r = lax.rsqrt(row_sq / width + 1e-06)[:, None]
    u_slab = (x0 * r * gain[None, :]).astype(jnp.bfloat16)
    u = lax.all_gather(u_slab, "dp", axis=1, tiled=True)
    proj = jnp.einsum("td,jdc->tjc", u, w_in, preferred_element_type=f32).astype(jnp.bfloat16)
    head = shifted(proj[rows - (taps - 1) :], "ctx", 1)
    p_ext = jnp.concatenate([head, proj], axis=0)
    z = short_filter(p_ext, short_filt, rows)
    kv = (z[:, 1] * z[:, 2]).astype(jnp.bfloat16)
    kv_head = shifted(kv[rows - (span - 1) :], "ctx", 1)
    kv_ext = jnp.concatenate([kv_head, kv, jnp.zeros((1,) + kv.shape[1:], kv.dtype)], axis=0)
    q = z[:, 0]
    k = z[:, 1]
    v = z[:, 2]
    lags = jnp.arange(span).astype(f32)[:, None]
    decay = jnp.exp(-rates[None, :] * lags)
    taps_eff = mr_filt * decay
    kv_wide = kv_ext.astype(f32)

    m = medium_forward(kv_wide, taps_eff, rows)
    h = (q * m).astype(jnp.bfloat16)
    y_part = jnp.dot(h, w_out, preferred_element_type=f32)
    y = lax.psum_scatter(y_part, "dp", scatter_dimension=1, tiled=True)
    block_out = (x0 + y).astype(jnp.bfloat16)
    logits = lax.psum(jnp.dot(block_out, w_tag, preferred_element_type=f32), "dp")
    top = jnp.max(logits, axis=1)
    lse = top + jnp.log(jnp.sum(jnp.exp(logits - top[:, None]), axis=1))
    tag_hot = (tags[:, None] == jnp.arange(w_tag.shape[1])[None, :]).astype(f32)
    loss_part = jnp.sum(lse - jnp.sum(logits * tag_hot, axis=1))
    dlog = jnp.exp(logits - lse[:, None]) - tag_hot
    dout = jnp.dot(dlog, w_tag.astype(f32).T, precision=high)
    tag_part = jnp.dot(block_out.astype(f32).T, dlog, precision=high)
    dy = dout.astype(jnp.bfloat16)
    dy_full = lax.all_gather(dy, "dp", axis=1, tiled=True)
    dh = lax.dot_general(dy_full, w_out, (((1,), (1,)), ((), ())), preferred_element_type=f32)
    out_part = lax.dot_general(h, dy_full, (((0,), (0,)), ((), ())), preferred_element_type=f32)
    d_w_out = lax.psum_scatter(
        out_part.astype(jnp.bfloat16), "ctx", scatter_dimension=1, tiled=True
    ).astype(jnp.float32)
    dq = dh * m
    dm = dh * q
    dm_tail = shifted(dm[: span - 1].astype(jnp.bfloat16), "ctx", -1).astype(jnp.float32)
    dm_ext = jnp.concatenate([dm, dm_tail, jnp.zeros((1,) + dm.shape[1:], f32)], axis=0)
    dkv, corr = medium_backward(dm_ext, kv_wide, taps_eff, rows)
    mr_part = corr * decay
    rate_part = -jnp.sum(lags * mr_filt * mr_part, axis=0)
    dz = jnp.stack([dq, dkv * v, dkv * k], axis=1)
    dz_tail = shifted(dz[: taps - 1], "ctx", -1)
    dz_ext = jnp.concatenate([dz, dz_tail], axis=0)
    dp = jnp.zeros_like(dz)
    shorts = []
    for s in range(taps):
        dp = dp + short_filt[None, :, s, :] * dz_ext[s : s + rows]
        shorts.append(jnp.sum(dz * p_ext[taps - 1 - s : taps - 1 - s + rows].astype(f32), axis=0))
    short_part = jnp.stack(shorts, axis=1)
    dpb = dp.astype(jnp.bfloat16)
    in_part = jnp.einsum("td,tjc->jdc", u, dpb, preferred_element_type=f32)
    d_w_in = lax.psum_scatter(
        in_part.astype(jnp.bfloat16), "ctx", scatter_dimension=1, tiled=True
    ).astype(jnp.float32)
    du_part = jnp.einsum("tjc,jdc->td", dpb, w_in, preferred_element_type=f32)
    du = lax.psum_scatter(
        du_part.astype(jnp.bfloat16), "dp", scatter_dimension=1, tiled=True
    ).astype(jnp.float32)
    gain_part = jnp.sum(du * x0 * r, axis=0)
    dn = du * gain[None, :]
    row_dot = lax.psum(jnp.sum(dn * x0, axis=1), "dp")[:, None] / width
    dx0 = dout + r * (dn - x0 * r * r * row_dot)
    embed_part = jnp.dot(id_hot.astype(f32).T, dx0, precision=high)
    d_embed = lax.psum_scatter(embed_part, "ctx", scatter_dimension=0, tiled=True)
    totals = (
        lax.psum(loss_part.astype(jnp.bfloat16), "ctx").astype(jnp.float32),
        lax.psum(gain_part.astype(jnp.bfloat16), "ctx").astype(jnp.float32),
        lax.psum(short_part.astype(jnp.bfloat16), "ctx").astype(jnp.float32),
        lax.psum(mr_part.astype(jnp.bfloat16), "ctx").astype(jnp.float32),
        lax.psum(rate_part.astype(jnp.bfloat16), "ctx").astype(jnp.float32),
        lax.psum(tag_part.astype(jnp.bfloat16), "ctx").astype(jnp.float32),
    )
    loss = totals[0] / (rows * n_ctx)
    return (
        loss,
        block_out,
        d_embed,
        totals[1],
        d_w_in,
        totals[2],
        totals[3],
        totals[4],
        d_w_out,
        totals[5],
    )


def solution(mesh):
    placed = (
        P("ctx"),
        P("ctx"),
        P(None, "dp"),
        P("dp"),
        P(None, None, "dp"),
        P(None, None, "dp"),
        P(None, "dp"),
        P("dp"),
        P("dp", None),
        P("dp", None),
    )
    return jax.shard_map(
        body,
        mesh=mesh,
        in_specs=placed,
        out_specs=(
            P(),
            P("ctx", "dp"),
            P("ctx", "dp"),
            P("dp"),
            P(None, "ctx", "dp"),
            P(None, None, "dp"),
            P(None, "dp"),
            P("dp"),
            P("dp", "ctx"),
            P("dp", None),
        ),
        check_vma=False,
    )
```

```python
import jax
import jax.numpy as jnp
from jax import lax
from jax.sharding import PartitionSpec as P
from jax.experimental import pallas as pl
from jax.experimental.pallas import tpu as pltpu

LANES = 128
ROW_BLOCK = 64


def medium_forward(kv_ext, taps_eff, rows):
    span, width = taps_eff.shape

    def kernel(kv_ref, g_ref, m_ref):
        for rb in range(0, rows, ROW_BLOCK):
            acc = jnp.zeros((ROW_BLOCK, LANES), jnp.float32)
            for s in range(span):
                start = span - 1 - s + rb
                acc = acc + g_ref[s : s + 1, :] * kv_ref[start : start + ROW_BLOCK, :]
            m_ref[rb : rb + ROW_BLOCK, :] = acc

    ext = kv_ext.shape[0]
    return pl.pallas_call(
        kernel,
        out_shape=jax.ShapeDtypeStruct((rows, width), jnp.float32),
        grid=(width // LANES,),
        in_specs=[
            pl.BlockSpec((ext, LANES), lambda c: (0, c)),
            pl.BlockSpec((span, LANES), lambda c: (0, c)),
        ],
        out_specs=pl.BlockSpec((rows, LANES), lambda c: (0, c)),
    )(kv_ext, taps_eff)


def medium_backward(dm_ext, kv_ext, taps_eff, rows):
    span, width = taps_eff.shape

    def kernel(dm_ref, kv_ref, g_ref, dkv_ref, corr_ref):
        for rb in range(0, rows, ROW_BLOCK):
            acc = jnp.zeros((ROW_BLOCK, LANES), jnp.float32)
            for s in range(span):
                acc = acc + g_ref[s : s + 1, :] * dm_ref[s + rb : s + rb + ROW_BLOCK, :]
            dkv_ref[rb : rb + ROW_BLOCK, :] = acc
        for s0 in range(0, span, 8):
            parts = []
            for s in range(s0, s0 + 8):
                start = span - 1 - s
                part = jnp.zeros((8, LANES), jnp.float32)
                for rb in range(0, rows, 8):
                    part = part + dm_ref[rb : rb + 8, :] * kv_ref[start + rb : start + rb + 8, :]
                parts.append(jnp.sum(part, axis=0, keepdims=True))
            corr_ref[s0 : s0 + 8, :] = jnp.concatenate(parts, axis=0)

    ext = kv_ext.shape[0]
    return pl.pallas_call(
        kernel,
        out_shape=(
            jax.ShapeDtypeStruct((rows, width), jnp.float32),
            jax.ShapeDtypeStruct((span, width), jnp.float32),
        ),
        grid=(width // LANES,),
        in_specs=[
            pl.BlockSpec((dm_ext.shape[0], LANES), lambda c: (0, c)),
            pl.BlockSpec((ext, LANES), lambda c: (0, c)),
            pl.BlockSpec((span, LANES), lambda c: (0, c)),
        ],
        out_specs=(
            pl.BlockSpec((rows, LANES), lambda c: (0, c)),
            pl.BlockSpec((span, LANES), lambda c: (0, c)),
        ),
    )(dm_ext, kv_ext, taps_eff)


def shifted(block, axis, distance):
    devices = range(lax.axis_size(axis))
    route = [(i - distance, i) for i in devices if i - distance in devices]
    return lax.ppermute(block, axis, route)


def short_filter(padded, filters, count):
    taps = filters.shape[1]
    total = jnp.zeros((count,) + padded.shape[1:], jnp.float32)
    for s in range(taps):
        total = total + filters[None, :, s, :] * padded[taps - 1 - s : taps - 1 - s + count].astype(
            jnp.float32
        )
    return total


def split3(x):
    parts = []
    rest = x
    for _ in range(3):
        part = lax.reduce_precision(rest, exponent_bits=8, mantissa_bits=7)
        parts.append(part)
        rest = rest - part
    return [p.astype(jnp.bfloat16) for p in parts]


def split2(x):
    hi = lax.reduce_precision(x, exponent_bits=8, mantissa_bits=7)
    return [hi.astype(jnp.bfloat16), (x - hi).astype(jnp.bfloat16)]


def as_rows(flat, width):
    pad = (-flat.shape[0]) % width
    return jnp.pad(flat, (0, pad)).reshape(-1, width)


def body(ids, tags, embed, gain, w_in, short_filt, mr_filt, rates, w_out, w_tag):
    f32 = jnp.float32
    bf16 = jnp.bfloat16
    high = lax.Precision.HIGHEST
    rows = ids.shape[0]
    vocab = embed.shape[0]
    cw = embed.shape[1]
    width = w_in.shape[1]
    taps = short_filt.shape[1]
    span = mr_filt.shape[0]
    n_tags = w_tag.shape[1]
    n_ctx = lax.axis_size("ctx")
    k_ctx = lax.axis_index("ctx")
    seq = rows * n_ctx

    packed = jnp.concatenate([embed, jnp.stack(split3(gain), axis=0), w_tag.T], axis=0)
    packed_full = lax.all_gather(packed, "dp", axis=1, tiled=True)
    w_out_cols = lax.all_to_all(w_out, "dp", 1, 0, tiled=True)
    packed_full, w_out_cols = lax.optimization_barrier((packed_full, w_out_cols))
    embed_full = packed_full[:vocab]
    gain_full = (
        packed_full[vocab].astype(f32) + packed_full[vocab + 1].astype(f32)
    ) + packed_full[vocab + 2].astype(f32)
    w_tag_full_t = packed_full[vocab + 3 : vocab + 3 + n_tags].astype(f32)

    emb32 = embed_full.astype(f32)
    r_vocab = lax.rsqrt(jnp.sum(emb32 * emb32, axis=1) / width + 1e-06)
    vocab_ids = jnp.arange(vocab)
    id_mask = ids[:, None] == vocab_ids[None, :]
    id_hot = id_mask.astype(bf16)
    r = jnp.sum(jnp.where(id_mask, r_vocab[None, :], 0.0), axis=1)[:, None]
    x0_full = jnp.dot(id_hot, embed_full, preferred_element_type=f32)
    x0 = jnp.dot(id_hot, embed, preferred_element_type=f32)
    u = (x0_full * r * gain_full[None, :]).astype(bf16)
    proj = jnp.einsum("td,jdc->tjc", u, w_in, preferred_element_type=f32).astype(bf16)
    head = shifted(proj[rows - (taps - 1) :], "ctx", 1)
    p_ext = jnp.concatenate([head, proj], axis=0)
    z = short_filter(p_ext, short_filt, rows)
    kv = (z[:, 1] * z[:, 2]).astype(bf16)
    kv_head = shifted(kv[rows - (span - 1) :], "ctx", 1)
    kv_ext = jnp.concatenate([kv_head, kv, jnp.zeros((1,) + kv.shape[1:], kv.dtype)], axis=0)
    q = z[:, 0]
    k = z[:, 1]
    v = z[:, 2]
    lags = jnp.arange(span).astype(f32)[:, None]
    decay = jnp.exp(-rates[None, :] * lags)
    taps_eff = mr_filt * decay
    kv_wide = kv_ext.astype(f32)
    m = medium_forward(kv_wide, taps_eff, rows)
    h = (q * m).astype(bf16)
    h_full = lax.all_gather(h, "dp", axis=1, tiled=True)
    y = jnp.dot(h_full, w_out_cols, preferred_element_type=f32)
    block_out = (x0 + y).astype(bf16)
    id_hi = (ids // 32).astype(bf16)
    id_lo = (ids % 32).astype(bf16)
    h_ids = jnp.concatenate([h, as_rows(jnp.concatenate([id_hi, id_lo]), cw)], axis=0)
    h_ids_all = lax.all_gather(h_ids, "ctx", axis=0, tiled=True).reshape(n_ctx, -1, cw)
    logits = lax.psum(jnp.dot(block_out, w_tag, preferred_element_type=f32), "dp")
    top = jnp.max(logits, axis=1)
    lse = top + jnp.log(jnp.sum(jnp.exp(logits - top[:, None]), axis=1))
    tag_hot = (tags[:, None] == jnp.arange(n_tags)[None, :]).astype(f32)
    loss_part = jnp.sum(lse - jnp.sum(logits * tag_hot, axis=1))
    dlog = jnp.exp(logits - lse[:, None]) - tag_hot
    dout = jnp.dot(dlog, w_tag.astype(f32).T, precision=high)
    tag_part = jnp.dot(block_out.astype(f32).T, dlog, precision=high)
    dy_full = jnp.dot(dlog, w_tag_full_t, precision=high).astype(bf16)
    dh = lax.dot_general(dy_full, w_out, (((1,), (1,)), ((), ())), preferred_element_type=f32)
    dq = dh * m
    dm = dh * q
    dm_tail = shifted(dm[: span - 1].astype(bf16), "ctx", -1).astype(f32)
    dm_ext = jnp.concatenate([dm, dm_tail, jnp.zeros((1,) + dm.shape[1:], f32)], axis=0)
    dkv, corr = medium_backward(dm_ext, kv_wide, taps_eff, rows)
    mr_part = corr * decay
    rate_part = -jnp.sum(lags * mr_filt * mr_part, axis=0)
    dz = jnp.stack([dq, dkv * v, dkv * k], axis=1)
    dz_tail = shifted(dz[: taps - 1], "ctx", -1)
    dz_ext = jnp.concatenate([dz, dz_tail], axis=0)
    dp = jnp.zeros_like(dz)
    shorts = []
    for s in range(taps):
        dp = dp + short_filt[None, :, s, :] * dz_ext[s : s + rows]
        shorts.append(jnp.sum(dz * p_ext[taps - 1 - s : taps - 1 - s + rows].astype(f32), axis=0))
    short_part = jnp.stack(shorts, axis=1)
    dpb = dp.astype(bf16)
    du_part = jnp.einsum("tjc,jdc->td", dpb, w_in, preferred_element_type=f32)
    du_part, h_ids_all = lax.optimization_barrier((du_part, h_ids_all))
    dot_part = jnp.sum(du_part * gain_full[None, :] * x0_full, axis=1)
    row_dot = lax.psum(dot_part, "dp")[:, None] / width
    du = lax.psum_scatter(du_part.astype(bf16), "dp", scatter_dimension=1, tiled=True).astype(f32)
    gain_part = jnp.sum(du * x0 * r, axis=0)
    dn = du * gain[None, :]
    dx0 = dout + r * (dn - x0 * r * r * row_dot)

    small = jnp.concatenate(
        [
            gain_part,
            short_part.reshape(-1),
            mr_part.reshape(-1),
            rate_part,
            tag_part.reshape(-1),
            loss_part[None],
        ]
    )
    n_small = small.shape[0]
    dlog_parts = split2(dlog.reshape(-1))
    tail = jnp.concatenate([small.astype(bf16)] + dlog_parts)
    final = jnp.concatenate(
        [jnp.transpose(dpb, (1, 0, 2)).reshape(-1, cw), dx0.astype(bf16), as_rows(tail, cw)],
        axis=0,
    )
    final_all = lax.all_gather(final, "ctx", axis=0, tiled=True).reshape(n_ctx, -1, cw)
    n_proj = 3 * rows
    dp_all = final_all[:, :n_proj].reshape(n_ctx, 3, rows, cw)
    dp_all = jnp.transpose(dp_all, (0, 2, 1, 3)).reshape(seq, 3, cw)
    dx0_all = final_all[:, n_proj : n_proj + rows].reshape(seq, cw).astype(f32)
    tail_all = final_all[:, n_proj + rows :].reshape(n_ctx, -1).astype(f32)
    small_tot = jnp.sum(tail_all[:, :n_small], axis=0)
    n_dlog = rows * n_tags
    dlog_all = (
        tail_all[:, n_small : n_small + n_dlog] + tail_all[:, n_small + n_dlog : n_small + 2 * n_dlog]
    ).reshape(seq, n_tags)

    h_all = h_ids_all[:, :rows].reshape(seq, cw)
    id_rows = h_ids_all[:, rows:].reshape(n_ctx, -1).astype(jnp.int32)
    ids_all = (id_rows[:, :rows] * 32 + id_rows[:, rows : 2 * rows]).reshape(seq)

    f_cols = width // n_ctx
    w_tag_cols = lax.dynamic_slice_in_dim(w_tag_full_t, k_ctx * f_cols, f_cols, 1)
    dy_all = jnp.dot(dlog_all, w_tag_cols, precision=high).astype(bf16)
    d_w_out = lax.dot_general(h_all, dy_all, (((0,), (0,)), ((), ())), preferred_element_type=f32)

    all_mask = ids_all[:, None] == vocab_ids[None, :]
    all_hot = all_mask.astype(bf16)
    r_all = jnp.sum(jnp.where(all_mask, r_vocab[None, :], 0.0), axis=1)[:, None]
    embed_k = lax.dynamic_slice_in_dim(embed_full, k_ctx * f_cols, f_cols, 1)
    gain_k = lax.dynamic_slice_in_dim(gain_full, k_ctx * f_cols, f_cols, 0)
    x0_k = jnp.dot(all_hot, embed_k, preferred_element_type=f32)
    u_k = (x0_k * r_all * gain_k[None, :]).astype(bf16)
    d_w_in = jnp.einsum("td,tjc->jdc", u_k, dp_all, preferred_element_type=f32)

    v_rows = vocab // n_ctx
    own_hot = (ids_all[:, None] == (k_ctx * v_rows + jnp.arange(v_rows))[None, :]).astype(f32)
    d_embed = jnp.dot(own_hot.T, dx0_all, precision=high)

    pos = 0
    outs = []
    for size, shape in (
        (cw, (cw,)),
        (3 * taps * cw, (3, taps, cw)),
        (span * cw, (span, cw)),
        (cw, (cw,)),
        (cw * n_tags, (cw, n_tags)),
        (1, ()),
    ):
        outs.append(small_tot[pos : pos + size].reshape(shape))
        pos += size
    gain_tot, short_tot, mr_tot, rate_tot, tag_tot, loss_tot = outs
    loss = loss_tot / seq
    return (
        loss,
        block_out,
        d_embed,
        gain_tot,
        d_w_in,
        short_tot,
        mr_tot,
        rate_tot,
        d_w_out,
        tag_tot,
    )


def solution(mesh):
    placed = (
        P("ctx"),
        P("ctx"),
        P(None, "dp"),
        P("dp"),
        P(None, None, "dp"),
        P(None, None, "dp"),
        P(None, "dp"),
        P("dp"),
        P("dp", None),
        P("dp", None),
    )
    return jax.shard_map(
        body,
        mesh=mesh,
        in_specs=placed,
        out_specs=(
            P(),
            P("ctx", "dp"),
            P("ctx", "dp"),
            P("dp"),
            P(None, "ctx", "dp"),
            P(None, None, "dp"),
            P(None, "dp"),
            P("dp"),
            P("dp", "ctx"),
            P("dp", None),
        ),
        check_vma=False,
    )
```

```python
import jax
import jax.numpy as jnp
from jax import lax
from jax.sharding import PartitionSpec as P
from jax.experimental import pallas as pl

LANES = 128
ROW_BLOCK = 64


def medium_forward(kv_ext, taps_eff, rows):
    span, width = taps_eff.shape

    def kernel(kv_ref, g_ref, m_ref):
        for rb in range(0, rows, ROW_BLOCK):
            acc = jnp.zeros((ROW_BLOCK, LANES), jnp.float32)
            for s in range(span):
                start = span - 1 - s + rb
                acc = acc + g_ref[s : s + 1, :] * kv_ref[start : start + ROW_BLOCK, :]
            m_ref[rb : rb + ROW_BLOCK, :] = acc

    ext = kv_ext.shape[0]
    return pl.pallas_call(
        kernel,
        out_shape=jax.ShapeDtypeStruct((rows, width), jnp.float32),
        grid=(width // LANES,),
        in_specs=[
            pl.BlockSpec((ext, LANES), lambda c: (0, c)),
            pl.BlockSpec((span, LANES), lambda c: (0, c)),
        ],
        out_specs=pl.BlockSpec((rows, LANES), lambda c: (0, c)),
    )(kv_ext, taps_eff)


def medium_backward(dm_ext, kv_ext, taps_eff, rows):
    span, width = taps_eff.shape

    def kernel(dm_ref, kv_ref, g_ref, dkv_ref, corr_ref):
        for rb in range(0, rows, ROW_BLOCK):
            acc = jnp.zeros((ROW_BLOCK, LANES), jnp.float32)
            for s in range(span):
                acc = acc + g_ref[s : s + 1, :] * dm_ref[s + rb : s + rb + ROW_BLOCK, :]
            dkv_ref[rb : rb + ROW_BLOCK, :] = acc
        for s0 in range(0, span, 8):
            parts = []
            for s in range(s0, s0 + 8):
                start = span - 1 - s
                part = jnp.zeros((8, LANES), jnp.float32)
                for rb in range(0, rows, 8):
                    part = part + dm_ref[rb : rb + 8, :] * kv_ref[start + rb : start + rb + 8, :]
                parts.append(jnp.sum(part, axis=0, keepdims=True))
            corr_ref[s0 : s0 + 8, :] = jnp.concatenate(parts, axis=0)

    ext = kv_ext.shape[0]
    return pl.pallas_call(
        kernel,
        out_shape=(
            jax.ShapeDtypeStruct((rows, width), jnp.float32),
            jax.ShapeDtypeStruct((span, width), jnp.float32),
        ),
        grid=(width // LANES,),
        in_specs=[
            pl.BlockSpec((dm_ext.shape[0], LANES), lambda c: (0, c)),
            pl.BlockSpec((ext, LANES), lambda c: (0, c)),
            pl.BlockSpec((span, LANES), lambda c: (0, c)),
        ],
        out_specs=(
            pl.BlockSpec((rows, LANES), lambda c: (0, c)),
            pl.BlockSpec((span, LANES), lambda c: (0, c)),
        ),
    )(dm_ext, kv_ext, taps_eff)


def shifted(block, axis, distance):
    devices = range(lax.axis_size(axis))
    route = [(i - distance, i) for i in devices if i - distance in devices]
    return lax.ppermute(block, axis, route)


def short_filter(padded, filters, count):
    taps = filters.shape[1]
    total = jnp.zeros((count,) + padded.shape[1:], jnp.float32)
    for s in range(taps):
        total = total + filters[None, :, s, :] * padded[taps - 1 - s : taps - 1 - s + count].astype(
            jnp.float32
        )
    return total


def split3(x):
    parts = []
    rest = x
    for _ in range(3):
        part = lax.reduce_precision(rest, exponent_bits=8, mantissa_bits=7)
        parts.append(part)
        rest = rest - part
    return [p.astype(jnp.bfloat16) for p in parts]


def split2(x):
    hi = lax.reduce_precision(x, exponent_bits=8, mantissa_bits=7)
    return [hi.astype(jnp.bfloat16), (x - hi).astype(jnp.bfloat16)]


def as_rows(flat, width):
    pad = (-flat.shape[0]) % width
    return jnp.pad(flat, (0, pad)).reshape(-1, width)


def block(ids, tags, embed, gain, w_in, short_filt, mr_filt, rates, w_out, w_tag):
    f32 = jnp.float32
    bf16 = jnp.bfloat16
    high = lax.Precision.HIGHEST
    rows = ids.shape[0]
    vocab = embed.shape[0]
    cw = embed.shape[1]
    width = w_in.shape[1]
    taps = short_filt.shape[1]
    span = mr_filt.shape[0]
    n_tags = w_tag.shape[1]
    n_ctx = lax.axis_size("ctx")
    k_ctx = lax.axis_index("ctx")
    seq = rows * n_ctx

    packed = jnp.concatenate([embed, jnp.stack(split3(gain), axis=0), w_tag.T], axis=0)
    packed_full = lax.all_gather(packed, "dp", axis=1, tiled=True)
    w_out_cols = lax.all_to_all(w_out, "dp", 1, 0, tiled=True)
    packed_full, w_out_cols = lax.optimization_barrier((packed_full, w_out_cols))
    embed_full = packed_full[:vocab]
    gain_full = (
        packed_full[vocab].astype(f32) + packed_full[vocab + 1].astype(f32)
    ) + packed_full[vocab + 2].astype(f32)
    w_tag_full_t = packed_full[vocab + 3 : vocab + 3 + n_tags].astype(f32)

    emb32 = embed_full.astype(f32)
    r_vocab = lax.rsqrt(jnp.sum(emb32 * emb32, axis=1) / width + 1e-06)
    vocab_ids = jnp.arange(vocab)
    id_mask = ids[:, None] == vocab_ids[None, :]
    id_hot = id_mask.astype(bf16)
    r = jnp.sum(jnp.where(id_mask, r_vocab[None, :], 0.0), axis=1)[:, None]
    x0_full = jnp.dot(id_hot, embed_full, preferred_element_type=f32)
    x0 = jnp.dot(id_hot, embed, preferred_element_type=f32)
    u = (x0_full * r * gain_full[None, :]).astype(bf16)
    proj = jnp.einsum("td,jdc->tjc", u, w_in, preferred_element_type=f32).astype(bf16)
    head = shifted(proj[rows - (taps - 1) :], "ctx", 1)
    p_ext = jnp.concatenate([head, proj], axis=0)
    z = short_filter(p_ext, short_filt, rows)
    kv = (z[:, 1] * z[:, 2]).astype(bf16)
    kv_head = shifted(kv[rows - (span - 1) :], "ctx", 1)
    kv_ext = jnp.concatenate([kv_head, kv, jnp.zeros((1,) + kv.shape[1:], kv.dtype)], axis=0)
    q = z[:, 0]
    k = z[:, 1]
    v = z[:, 2]
    lags = jnp.arange(span).astype(f32)[:, None]
    decay = jnp.exp(-rates[None, :] * lags)
    taps_eff = mr_filt * decay
    kv_wide = kv_ext.astype(f32)
    m = medium_forward(kv_wide, taps_eff, rows)
    h = (q * m).astype(bf16)
    h_full = lax.all_gather(h, "dp", axis=1, tiled=True)
    y = jnp.dot(h_full, w_out_cols, preferred_element_type=f32)
    block_out = (x0 + y).astype(bf16)
    id_hi = (ids // 32).astype(bf16)
    id_lo = (ids % 32).astype(bf16)
    h_ids = jnp.concatenate([h, as_rows(jnp.concatenate([id_hi, id_lo]), cw)], axis=0)
    h_ids_all = lax.all_gather(h_ids, "ctx", axis=0, tiled=True).reshape(n_ctx, -1, cw)
    logits = lax.psum(jnp.dot(block_out, w_tag, preferred_element_type=f32), "dp")
    top = jnp.max(logits, axis=1)
    lse = top + jnp.log(jnp.sum(jnp.exp(logits - top[:, None]), axis=1))
    tag_hot = (tags[:, None] == jnp.arange(n_tags)[None, :]).astype(f32)
    loss_part = jnp.sum(lse - jnp.sum(logits * tag_hot, axis=1))
    dlog = jnp.exp(logits - lse[:, None]) - tag_hot
    dout = jnp.dot(dlog, w_tag.astype(f32).T, precision=high)
    tag_part = jnp.dot(block_out.astype(f32).T, dlog, precision=high)
    dy_full = jnp.dot(dlog, w_tag_full_t, precision=high).astype(bf16)
    dh = lax.dot_general(dy_full, w_out, (((1,), (1,)), ((), ())), preferred_element_type=f32)
    dq = dh * m
    dm = dh * q
    dm_tail = shifted(dm[: span - 1].astype(bf16), "ctx", -1).astype(f32)
    dm_ext = jnp.concatenate([dm, dm_tail, jnp.zeros((1,) + dm.shape[1:], f32)], axis=0)
    dkv, corr = medium_backward(dm_ext, kv_wide, taps_eff, rows)
    mr_part = corr * decay
    rate_part = -jnp.sum(lags * mr_filt * mr_part, axis=0)
    dz = jnp.stack([dq, dkv * v, dkv * k], axis=1)
    dz_tail = shifted(dz[: taps - 1], "ctx", -1)
    dz_ext = jnp.concatenate([dz, dz_tail], axis=0)
    dp = jnp.zeros_like(dz)
    shorts = []
    for s in range(taps):
        dp = dp + short_filt[None, :, s, :] * dz_ext[s : s + rows]
        shorts.append(jnp.sum(dz * p_ext[taps - 1 - s : taps - 1 - s + rows].astype(f32), axis=0))
    short_part = jnp.stack(shorts, axis=1)
    dpb = dp.astype(bf16)
    dp_all = lax.all_gather(jnp.transpose(dpb, (1, 0, 2)), "ctx", axis=1, tiled=True)
    du_part = jnp.einsum("tjc,jdc->td", dpb, w_in, preferred_element_type=f32)
    du_part, h_ids_all = lax.optimization_barrier((du_part, h_ids_all))
    dot_part = jnp.sum(du_part * gain_full[None, :] * x0_full, axis=1)
    row_dot = lax.psum(dot_part, "dp")[:, None] / width
    n_dp = lax.axis_size("dp")
    du_chunks = lax.all_to_all(du_part.astype(bf16), "dp", 1, 0, tiled=True)
    du = jnp.sum(du_chunks.reshape(n_dp, rows, cw).astype(f32), axis=0)
    gain_part = jnp.sum(du * x0 * r, axis=0)
    dn = du * gain[None, :]
    dx0 = dout + r * (dn - x0 * r * r * row_dot)

    small = jnp.concatenate(
        [
            gain_part,
            short_part.reshape(-1),
            mr_part.reshape(-1),
            rate_part,
            tag_part.reshape(-1),
            loss_part[None],
        ]
    )
    n_small = small.shape[0]
    dlog_parts = split2(dlog.reshape(-1))
    tail = jnp.concatenate([small.astype(bf16)] + dlog_parts)
    final = jnp.concatenate(
        [dx0.astype(bf16), as_rows(tail, cw)],
        axis=0,
    )
    final_all = lax.all_gather(final, "ctx", axis=0, tiled=True).reshape(n_ctx, -1, cw)
    dx0_all = final_all[:, :rows].reshape(seq, cw).astype(f32)
    tail_all = final_all[:, rows:].reshape(n_ctx, -1).astype(f32)
    small_tot = jnp.sum(tail_all[:, :n_small], axis=0)
    n_dlog = rows * n_tags
    dlog_all = (
        tail_all[:, n_small : n_small + n_dlog] + tail_all[:, n_small + n_dlog : n_small + 2 * n_dlog]
    ).reshape(seq, n_tags)

    h_all = h_ids_all[:, :rows].reshape(seq, cw)
    id_rows = h_ids_all[:, rows:].reshape(n_ctx, -1).astype(jnp.int32)
    ids_all = (id_rows[:, :rows] * 32 + id_rows[:, rows : 2 * rows]).reshape(seq)

    f_cols = width // n_ctx
    w_tag_cols = lax.dynamic_slice_in_dim(w_tag_full_t, k_ctx * f_cols, f_cols, 1)
    dy_all = jnp.dot(dlog_all, w_tag_cols, precision=high).astype(bf16)
    d_w_out = lax.dot_general(h_all, dy_all, (((0,), (0,)), ((), ())), preferred_element_type=f32)

    all_mask = ids_all[:, None] == vocab_ids[None, :]
    all_hot = all_mask.astype(bf16)
    r_all = jnp.sum(jnp.where(all_mask, r_vocab[None, :], 0.0), axis=1)[:, None]
    embed_k = lax.dynamic_slice_in_dim(embed_full, k_ctx * f_cols, f_cols, 1)
    gain_k = lax.dynamic_slice_in_dim(gain_full, k_ctx * f_cols, f_cols, 0)
    x0_k = jnp.dot(all_hot, embed_k, preferred_element_type=f32)
    u_k = (x0_k * r_all * gain_k[None, :]).astype(bf16)
    d_w_in = jnp.einsum("td,jtc->jdc", u_k, dp_all, preferred_element_type=f32)

    v_rows = vocab // n_ctx
    own_hot = (ids_all[:, None] == (k_ctx * v_rows + jnp.arange(v_rows))[None, :]).astype(f32)
    d_embed = jnp.dot(own_hot.T, dx0_all, precision=high)

    pos = 0
    outs = []
    for size, shape in (
        (cw, (cw,)),
        (3 * taps * cw, (3, taps, cw)),
        (span * cw, (span, cw)),
        (cw, (cw,)),
        (cw * n_tags, (cw, n_tags)),
        (1, ()),
    ):
        outs.append(small_tot[pos : pos + size].reshape(shape))
        pos += size
    gain_tot, short_tot, mr_tot, rate_tot, tag_tot, loss_tot = outs
    loss = loss_tot / seq
    return (
        loss,
        block_out,
        d_embed,
        gain_tot,
        d_w_in,
        short_tot,
        mr_tot,
        rate_tot,
        d_w_out,
        tag_tot,
    )


def solution(mesh):
    placed = (
        P("ctx"),
        P("ctx"),
        P(None, "dp"),
        P("dp"),
        P(None, None, "dp"),
        P(None, None, "dp"),
        P(None, "dp"),
        P("dp"),
        P("dp", None),
        P("dp", None),
    )
    return jax.shard_map(
        block,
        mesh=mesh,
        in_specs=placed,
        out_specs=(
            P(),
            P("ctx", "dp"),
            P("ctx", "dp"),
            P("dp"),
            P(None, "ctx", "dp"),
            P(None, None, "dp"),
            P(None, "dp"),
            P("dp"),
            P("dp", "ctx"),
            P("dp", None),
        ),
        check_vma=False,
    )
```

```python
import jax
import jax.numpy as jnp
from jax import lax
from jax.sharding import PartitionSpec as P
from jax.experimental import pallas as pl

LANES = 128
ROW_BLOCK = 64


def medium_forward(kv_ext, taps_eff, rows):
    span, width = taps_eff.shape

    def kernel(kv_ref, g_ref, m_ref):
        for rb in range(0, rows, ROW_BLOCK):
            acc = jnp.zeros((ROW_BLOCK, LANES), jnp.float32)
            for s in range(span):
                start = span - 1 - s + rb
                acc = acc + g_ref[s : s + 1, :] * kv_ref[start : start + ROW_BLOCK, :]
            m_ref[rb : rb + ROW_BLOCK, :] = acc

    ext = kv_ext.shape[0]
    return pl.pallas_call(
        kernel,
        out_shape=jax.ShapeDtypeStruct((rows, width), jnp.float32),
        grid=(width // LANES,),
        in_specs=[
            pl.BlockSpec((ext, LANES), lambda c: (0, c)),
            pl.BlockSpec((span, LANES), lambda c: (0, c)),
        ],
        out_specs=pl.BlockSpec((rows, LANES), lambda c: (0, c)),
    )(kv_ext, taps_eff)


def medium_backward(dm_ext, kv_ext, taps_eff, rows):
    span, width = taps_eff.shape

    def kernel(dm_ref, kv_ref, g_ref, dkv_ref, corr_ref):
        for rb in range(0, rows, ROW_BLOCK):
            acc = jnp.zeros((ROW_BLOCK, LANES), jnp.float32)
            for s in range(span):
                acc = acc + g_ref[s : s + 1, :] * dm_ref[s + rb : s + rb + ROW_BLOCK, :]
            dkv_ref[rb : rb + ROW_BLOCK, :] = acc
        for s0 in range(0, span, 8):
            parts = []
            for s in range(s0, s0 + 8):
                start = span - 1 - s
                part = jnp.zeros((8, LANES), jnp.float32)
                for rb in range(0, rows, 8):
                    part = part + dm_ref[rb : rb + 8, :] * kv_ref[start + rb : start + rb + 8, :]
                parts.append(jnp.sum(part, axis=0, keepdims=True))
            corr_ref[s0 : s0 + 8, :] = jnp.concatenate(parts, axis=0)

    ext = kv_ext.shape[0]
    return pl.pallas_call(
        kernel,
        out_shape=(
            jax.ShapeDtypeStruct((rows, width), jnp.float32),
            jax.ShapeDtypeStruct((span, width), jnp.float32),
        ),
        grid=(width // LANES,),
        in_specs=[
            pl.BlockSpec((dm_ext.shape[0], LANES), lambda c: (0, c)),
            pl.BlockSpec((ext, LANES), lambda c: (0, c)),
            pl.BlockSpec((span, LANES), lambda c: (0, c)),
        ],
        out_specs=(
            pl.BlockSpec((rows, LANES), lambda c: (0, c)),
            pl.BlockSpec((span, LANES), lambda c: (0, c)),
        ),
    )(dm_ext, kv_ext, taps_eff)


def shifted(block, axis, distance):
    devices = range(lax.axis_size(axis))
    route = [(i - distance, i) for i in devices if i - distance in devices]
    return lax.ppermute(block, axis, route)


def short_filter(padded, filters, count):
    taps = filters.shape[1]
    total = jnp.zeros((count,) + padded.shape[1:], jnp.float32)
    for s in range(taps):
        total = total + filters[None, :, s, :] * padded[taps - 1 - s : taps - 1 - s + count].astype(
            jnp.float32
        )
    return total


def split3(x):
    parts = []
    rest = x
    for _ in range(3):
        part = lax.reduce_precision(rest, exponent_bits=8, mantissa_bits=7)
        parts.append(part)
        rest = rest - part
    return [p.astype(jnp.bfloat16) for p in parts]


def split2(x):
    hi = lax.reduce_precision(x, exponent_bits=8, mantissa_bits=7)
    return [hi.astype(jnp.bfloat16), (x - hi).astype(jnp.bfloat16)]


def as_rows(flat, width):
    pad = (-flat.shape[0]) % width
    return jnp.pad(flat, (0, pad)).reshape(-1, width)


def block(ids, tags, embed, gain, w_in, short_filt, mr_filt, rates, w_out, w_tag):
    f32 = jnp.float32
    bf16 = jnp.bfloat16
    high = lax.Precision.HIGHEST
    rows = ids.shape[0]
    vocab = embed.shape[0]
    cw = embed.shape[1]
    width = w_in.shape[1]
    taps = short_filt.shape[1]
    span = mr_filt.shape[0]
    n_tags = w_tag.shape[1]
    n_ctx = lax.axis_size("ctx")
    k_ctx = lax.axis_index("ctx")
    seq = rows * n_ctx

    packed = jnp.concatenate([embed, jnp.stack(split3(gain), axis=0), w_tag.T], axis=0)
    packed_full = lax.all_gather(packed, "dp", axis=1, tiled=True)
    w_out_cols = lax.all_to_all(w_out, "dp", 1, 0, tiled=True)
    packed_full, w_out_cols = lax.optimization_barrier((packed_full, w_out_cols))
    embed_full = packed_full[:vocab]
    gain_full = (
        packed_full[vocab].astype(f32) + packed_full[vocab + 1].astype(f32)
    ) + packed_full[vocab + 2].astype(f32)
    w_tag_full_t = packed_full[vocab + 3 : vocab + 3 + n_tags].astype(f32)

    emb32 = embed_full.astype(f32)
    r_vocab = lax.rsqrt(jnp.sum(emb32 * emb32, axis=1) / width + 1e-06)
    vocab_ids = jnp.arange(vocab)
    id_mask = ids[:, None] == vocab_ids[None, :]
    id_hot = id_mask.astype(bf16)
    r = jnp.sum(jnp.where(id_mask, r_vocab[None, :], 0.0), axis=1)[:, None]
    x0_full = jnp.dot(id_hot, embed_full, preferred_element_type=f32)
    x0 = jnp.dot(id_hot, embed, preferred_element_type=f32)
    u = (x0_full * r * gain_full[None, :]).astype(bf16)
    proj = jnp.einsum("td,jdc->tjc", u, w_in, preferred_element_type=f32).astype(bf16)
    head = shifted(proj[rows - (taps - 1) :], "ctx", 1)
    p_ext = jnp.concatenate([head, proj], axis=0)
    z = short_filter(p_ext, short_filt, rows)
    kv = (z[:, 1] * z[:, 2]).astype(bf16)
    kv_head = shifted(kv[rows - (span - 1) :], "ctx", 1)
    kv_ext = jnp.concatenate([kv_head, kv, jnp.zeros((1,) + kv.shape[1:], kv.dtype)], axis=0)
    q = z[:, 0]
    k = z[:, 1]
    v = z[:, 2]
    lags = jnp.arange(span).astype(f32)[:, None]
    decay = jnp.exp(-rates[None, :] * lags)
    taps_eff = mr_filt * decay
    kv_wide = kv_ext.astype(f32)
    m = medium_forward(kv_wide, taps_eff, rows)
    h = (q * m).astype(bf16)
    h_full = lax.all_gather(h, "dp", axis=1, tiled=True)
    y = jnp.dot(h_full, w_out_cols, preferred_element_type=f32)
    block_out = (x0 + y).astype(bf16)
    id_hi = (ids // 32).astype(bf16)
    id_lo = (ids % 32).astype(bf16)
    h_ids = jnp.concatenate([h, as_rows(jnp.concatenate([id_hi, id_lo]), cw)], axis=0)
    h_ids_all = lax.all_gather(h_ids, "ctx", axis=0, tiled=True).reshape(n_ctx, -1, cw)
    logit_part = jnp.dot(block_out, w_tag, preferred_element_type=f32)
    n_dp = lax.axis_size("dp")
    logit_parts = lax.all_to_all(
        jnp.broadcast_to(logit_part[None], (n_dp,) + logit_part.shape), "dp", 0, 0, tiled=True
    )
    logits = jnp.sum(logit_parts, axis=0)
    top = jnp.max(logits, axis=1)
    lse = top + jnp.log(jnp.sum(jnp.exp(logits - top[:, None]), axis=1))
    tag_hot = (tags[:, None] == jnp.arange(n_tags)[None, :]).astype(f32)
    loss_part = jnp.sum(lse - jnp.sum(logits * tag_hot, axis=1))
    dlog = jnp.exp(logits - lse[:, None]) - tag_hot
    dout = jnp.dot(dlog, w_tag.astype(f32).T, precision=high)
    tag_part = jnp.dot(block_out.astype(f32).T, dlog, precision=high)
    dy_full = jnp.dot(dlog, w_tag_full_t, precision=high).astype(bf16)
    dh = lax.dot_general(dy_full, w_out, (((1,), (1,)), ((), ())), preferred_element_type=f32)
    dq = dh * m
    dm = dh * q
    dm_tail = shifted(dm[: span - 1].astype(bf16), "ctx", -1).astype(f32)
    dm_ext = jnp.concatenate([dm, dm_tail, jnp.zeros((1,) + dm.shape[1:], f32)], axis=0)
    dkv, corr = medium_backward(dm_ext, kv_wide, taps_eff, rows)
    mr_part = corr * decay
    rate_part = -jnp.sum(lags * mr_filt * mr_part, axis=0)
    dz = jnp.stack([dq, dkv * v, dkv * k], axis=1)
    dz_tail = shifted(dz[: taps - 1], "ctx", -1)
    dz_ext = jnp.concatenate([dz, dz_tail], axis=0)
    dp = jnp.zeros_like(dz)
    shorts = []
    for s in range(taps):
        dp = dp + short_filt[None, :, s, :] * dz_ext[s : s + rows]
        shorts.append(jnp.sum(dz * p_ext[taps - 1 - s : taps - 1 - s + rows].astype(f32), axis=0))
    short_part = jnp.stack(shorts, axis=1)
    dpb = dp.astype(bf16)
    dp_all = lax.all_gather(jnp.transpose(dpb, (1, 0, 2)), "ctx", axis=1, tiled=True)
    du_part = jnp.einsum("tjc,jdc->td", dpb, w_in, preferred_element_type=f32)
    du_part, h_ids_all = lax.optimization_barrier((du_part, h_ids_all))
    dot_part = jnp.sum(du_part * gain_full[None, :] * x0_full, axis=1)
    n_dp = lax.axis_size("dp")
    dot_rows = as_rows(jnp.concatenate(split2(dot_part)), cw)
    n_dot = dot_rows.shape[0]
    du_send = jnp.concatenate(
        [
            du_part.astype(bf16).reshape(rows, n_dp, cw),
            jnp.broadcast_to(dot_rows[:, None, :], (n_dot, n_dp, cw)),
        ],
        axis=0,
    )
    du_recv = lax.all_to_all(du_send, "dp", 1, 1, tiled=True).astype(f32)
    du = jnp.sum(du_recv[:rows], axis=1)
    dot_recv = jnp.sum(du_recv[rows:], axis=1).reshape(-1)
    row_dot = (dot_recv[:rows] + dot_recv[rows : 2 * rows])[:, None] / width
    gain_part = jnp.sum(du * x0 * r, axis=0)
    dn = du * gain[None, :]
    dx0 = dout + r * (dn - x0 * r * r * row_dot)

    small = jnp.concatenate(
        [
            gain_part,
            short_part.reshape(-1),
            mr_part.reshape(-1),
            rate_part,
            tag_part.reshape(-1),
            loss_part[None],
        ]
    )
    n_small = small.shape[0]
    dlog_parts = split2(dlog.reshape(-1))
    tail = jnp.concatenate([small.astype(bf16)] + dlog_parts)
    final = jnp.concatenate(
        [dx0.astype(bf16), as_rows(tail, cw)],
        axis=0,
    )
    final_all = lax.all_to_all(
        jnp.broadcast_to(final[None], (n_ctx,) + final.shape), "ctx", 0, 0, tiled=True
    )
    dx0_all = final_all[:, :rows].reshape(seq, cw).astype(f32)
    tail_all = final_all[:, rows:].reshape(n_ctx, -1).astype(f32)
    small_tot = jnp.sum(tail_all[:, :n_small], axis=0)
    n_dlog = rows * n_tags
    dlog_all = (
        tail_all[:, n_small : n_small + n_dlog] + tail_all[:, n_small + n_dlog : n_small + 2 * n_dlog]
    ).reshape(seq, n_tags)

    h_all = h_ids_all[:, :rows].reshape(seq, cw)
    id_rows = h_ids_all[:, rows:].reshape(n_ctx, -1).astype(jnp.int32)
    ids_all = (id_rows[:, :rows] * 32 + id_rows[:, rows : 2 * rows]).reshape(seq)

    f_cols = width // n_ctx
    w_tag_cols = lax.dynamic_slice_in_dim(w_tag_full_t, k_ctx * f_cols, f_cols, 1)
    dy_all = jnp.dot(dlog_all, w_tag_cols, precision=high).astype(bf16)
    d_w_out = lax.dot_general(h_all, dy_all, (((0,), (0,)), ((), ())), preferred_element_type=f32)

    all_mask = ids_all[:, None] == vocab_ids[None, :]
    all_hot = all_mask.astype(bf16)
    r_all = jnp.sum(jnp.where(all_mask, r_vocab[None, :], 0.0), axis=1)[:, None]
    embed_k = lax.dynamic_slice_in_dim(embed_full, k_ctx * f_cols, f_cols, 1)
    gain_k = lax.dynamic_slice_in_dim(gain_full, k_ctx * f_cols, f_cols, 0)
    x0_k = jnp.dot(all_hot, embed_k, preferred_element_type=f32)
    u_k = (x0_k * r_all * gain_k[None, :]).astype(bf16)
    d_w_in = jnp.einsum("td,jtc->jdc", u_k, dp_all, preferred_element_type=f32)

    v_rows = vocab // n_ctx
    own_hot = (ids_all[:, None] == (k_ctx * v_rows + jnp.arange(v_rows))[None, :]).astype(f32)
    d_embed = jnp.dot(own_hot.T, dx0_all, precision=high)

    pos = 0
    outs = []
    for size, shape in (
        (cw, (cw,)),
        (3 * taps * cw, (3, taps, cw)),
        (span * cw, (span, cw)),
        (cw, (cw,)),
        (cw * n_tags, (cw, n_tags)),
        (1, ()),
    ):
        outs.append(small_tot[pos : pos + size].reshape(shape))
        pos += size
    gain_tot, short_tot, mr_tot, rate_tot, tag_tot, loss_tot = outs
    loss = loss_tot / seq
    return (
        loss,
        block_out,
        d_embed,
        gain_tot,
        d_w_in,
        short_tot,
        mr_tot,
        rate_tot,
        d_w_out,
        tag_tot,
    )


def solution(mesh):
    placed = (
        P("ctx"),
        P("ctx"),
        P(None, "dp"),
        P("dp"),
        P(None, None, "dp"),
        P(None, None, "dp"),
        P(None, "dp"),
        P("dp"),
        P("dp", None),
        P("dp", None),
    )
    return jax.shard_map(
        block,
        mesh=mesh,
        in_specs=placed,
        out_specs=(
            P(),
            P("ctx", "dp"),
            P("ctx", "dp"),
            P("dp"),
            P(None, "ctx", "dp"),
            P(None, None, "dp"),
            P(None, "dp"),
            P("dp"),
            P("dp", "ctx"),
            P("dp", None),
        ),
        check_vma=False,
    )
```

```python
import jax
import jax.numpy as jnp
from jax import lax
from jax.sharding import PartitionSpec as P
from jax.experimental import pallas as pl

LANES = 128
ROW_BLOCK = 64


def medium_forward(kv_ext, taps_eff, rows):
    span, width = taps_eff.shape

    def kernel(kv_ref, g_ref, m_ref):
        for rb in range(0, rows, ROW_BLOCK):
            acc = jnp.zeros((ROW_BLOCK, LANES), jnp.float32)
            for s in range(span):
                start = span - 1 - s + rb
                acc = acc + g_ref[s : s + 1, :] * kv_ref[start : start + ROW_BLOCK, :]
            m_ref[rb : rb + ROW_BLOCK, :] = acc

    ext = kv_ext.shape[0]
    return pl.pallas_call(
        kernel,
        out_shape=jax.ShapeDtypeStruct((rows, width), jnp.float32),
        grid=(width // LANES,),
        in_specs=[
            pl.BlockSpec((ext, LANES), lambda c: (0, c)),
            pl.BlockSpec((span, LANES), lambda c: (0, c)),
        ],
        out_specs=pl.BlockSpec((rows, LANES), lambda c: (0, c)),
    )(kv_ext, taps_eff)


def medium_backward(dm_ext, kv_ext, taps_eff, rows):
    span, width = taps_eff.shape

    def kernel(dm_ref, kv_ref, g_ref, dkv_ref, corr_ref):
        for rb in range(0, rows, ROW_BLOCK):
            acc = jnp.zeros((ROW_BLOCK, LANES), jnp.float32)
            for s in range(span):
                acc = acc + g_ref[s : s + 1, :] * dm_ref[s + rb : s + rb + ROW_BLOCK, :]
            dkv_ref[rb : rb + ROW_BLOCK, :] = acc
        for s0 in range(0, span, 8):
            parts = []
            for s in range(s0, s0 + 8):
                start = span - 1 - s
                part = jnp.zeros((8, LANES), jnp.float32)
                for rb in range(0, rows, 8):
                    part = part + dm_ref[rb : rb + 8, :] * kv_ref[start + rb : start + rb + 8, :]
                parts.append(jnp.sum(part, axis=0, keepdims=True))
            corr_ref[s0 : s0 + 8, :] = jnp.concatenate(parts, axis=0)

    ext = kv_ext.shape[0]
    return pl.pallas_call(
        kernel,
        out_shape=(
            jax.ShapeDtypeStruct((rows, width), jnp.float32),
            jax.ShapeDtypeStruct((span, width), jnp.float32),
        ),
        grid=(width // LANES,),
        in_specs=[
            pl.BlockSpec((dm_ext.shape[0], LANES), lambda c: (0, c)),
            pl.BlockSpec((ext, LANES), lambda c: (0, c)),
            pl.BlockSpec((span, LANES), lambda c: (0, c)),
        ],
        out_specs=(
            pl.BlockSpec((rows, LANES), lambda c: (0, c)),
            pl.BlockSpec((span, LANES), lambda c: (0, c)),
        ),
    )(dm_ext, kv_ext, taps_eff)


def shifted(block, axis, distance):
    devices = range(lax.axis_size(axis))
    route = [(i - distance, i) for i in devices if i - distance in devices]
    return lax.ppermute(block, axis, route)


def short_filter(padded, filters, count):
    taps = filters.shape[1]
    total = jnp.zeros((count,) + padded.shape[1:], jnp.float32)
    for s in range(taps):
        total = total + filters[None, :, s, :] * padded[taps - 1 - s : taps - 1 - s + count].astype(
            jnp.float32
        )
    return total


def split3(x):
    parts = []
    rest = x
    for _ in range(3):
        part = lax.reduce_precision(rest, exponent_bits=8, mantissa_bits=7)
        parts.append(part)
        rest = rest - part
    return [p.astype(jnp.bfloat16) for p in parts]


def split2(x):
    hi = lax.reduce_precision(x, exponent_bits=8, mantissa_bits=7)
    return [hi.astype(jnp.bfloat16), (x - hi).astype(jnp.bfloat16)]


def as_rows(flat, width):
    pad = (-flat.shape[0]) % width
    return jnp.pad(flat, (0, pad)).reshape(-1, width)


def block(ids, tags, embed, gain, w_in, short_filt, mr_filt, rates, w_out, w_tag):
    f32 = jnp.float32
    bf16 = jnp.bfloat16
    high = lax.Precision.HIGHEST
    rows = ids.shape[0]
    vocab = embed.shape[0]
    cw = embed.shape[1]
    width = w_in.shape[1]
    taps = short_filt.shape[1]
    span = mr_filt.shape[0]
    n_tags = w_tag.shape[1]
    n_ctx = lax.axis_size("ctx")
    k_ctx = lax.axis_index("ctx")
    seq = rows * n_ctx

    n_dp = lax.axis_size("dp")
    half = vocab // 2
    packed = jnp.concatenate([embed[:half], jnp.stack(split3(gain), axis=0), w_tag.T], axis=0)
    packed_full = lax.all_gather(packed, "dp", axis=1, tiled=True)
    upper = lax.all_to_all(
        jnp.broadcast_to(embed[None, half:], (n_dp, vocab - half, cw)), "dp", 0, 0, tiled=True
    )
    upper_full = jnp.transpose(upper, (1, 0, 2)).reshape(vocab - half, width)
    w_out_later, upper_full = lax.optimization_barrier((w_out, upper_full))
    w_out_cols = lax.all_to_all(w_out_later, "dp", 1, 0, tiled=True)
    embed_full = jnp.concatenate([packed_full[:half], upper_full], axis=0)
    gain_full = (
        packed_full[half].astype(f32) + packed_full[half + 1].astype(f32)
    ) + packed_full[half + 2].astype(f32)
    w_tag_full_t = packed_full[half + 3 : half + 3 + n_tags].astype(f32)

    emb32 = embed_full.astype(f32)
    r_vocab = lax.rsqrt(jnp.sum(emb32 * emb32, axis=1) / width + 1e-06)
    vocab_ids = jnp.arange(vocab)
    id_mask = ids[:, None] == vocab_ids[None, :]
    id_hot = id_mask.astype(bf16)
    r = jnp.sum(jnp.where(id_mask, r_vocab[None, :], 0.0), axis=1)[:, None]
    x0_full = jnp.dot(id_hot, embed_full, preferred_element_type=f32)
    x0 = jnp.dot(id_hot, embed, preferred_element_type=f32)
    u = (x0_full * r * gain_full[None, :]).astype(bf16)
    proj = jnp.einsum("td,jdc->tjc", u, w_in, preferred_element_type=f32).astype(bf16)
    head = shifted(proj[rows - (taps - 1) :], "ctx", 1)
    p_ext = jnp.concatenate([head, proj], axis=0)
    z = short_filter(p_ext, short_filt, rows)
    kv = (z[:, 1] * z[:, 2]).astype(bf16)
    kv_head = shifted(kv[rows - (span - 1) :], "ctx", 1)
    kv_ext = jnp.concatenate([kv_head, kv, jnp.zeros((1,) + kv.shape[1:], kv.dtype)], axis=0)
    q = z[:, 0]
    k = z[:, 1]
    v = z[:, 2]
    lags = jnp.arange(span).astype(f32)[:, None]
    decay = jnp.exp(-rates[None, :] * lags)
    taps_eff = mr_filt * decay
    kv_wide = kv_ext.astype(f32)
    m = medium_forward(kv_wide, taps_eff, rows)
    h = (q * m).astype(bf16)
    h_full = lax.all_gather(h, "dp", axis=1, tiled=True)
    y = jnp.dot(h_full, w_out_cols, preferred_element_type=f32)
    block_out = (x0 + y).astype(bf16)
    id_hi = (ids // 32).astype(bf16)
    id_lo = (ids % 32).astype(bf16)
    h_ids = jnp.concatenate([h, as_rows(jnp.concatenate([id_hi, id_lo]), cw)], axis=0)
    h_ids_all = lax.all_gather(h_ids, "ctx", axis=0, tiled=True).reshape(n_ctx, -1, cw)
    logit_part = jnp.dot(block_out, w_tag, preferred_element_type=f32)
    logit_parts = lax.all_to_all(
        jnp.broadcast_to(logit_part[None], (n_dp,) + logit_part.shape), "dp", 0, 0, tiled=True
    )
    logits = jnp.sum(logit_parts, axis=0)
    top = jnp.max(logits, axis=1)
    lse = top + jnp.log(jnp.sum(jnp.exp(logits - top[:, None]), axis=1))
    tag_hot = (tags[:, None] == jnp.arange(n_tags)[None, :]).astype(f32)
    loss_part = jnp.sum(lse - jnp.sum(logits * tag_hot, axis=1))
    dlog = jnp.exp(logits - lse[:, None]) - tag_hot
    dout = jnp.dot(dlog, w_tag.astype(f32).T, precision=high)
    tag_part = jnp.dot(block_out.astype(f32).T, dlog, precision=high)
    dy_full = jnp.dot(dlog, w_tag_full_t, precision=high).astype(bf16)
    dh = lax.dot_general(dy_full, w_out, (((1,), (1,)), ((), ())), preferred_element_type=f32)
    dq = dh * m
    dm = dh * q
    dm_tail = shifted(dm[: span - 1].astype(bf16), "ctx", -1).astype(f32)
    dm_ext = jnp.concatenate([dm, dm_tail, jnp.zeros((1,) + dm.shape[1:], f32)], axis=0)
    dkv, corr = medium_backward(dm_ext, kv_wide, taps_eff, rows)
    mr_part = corr * decay
    rate_part = -jnp.sum(lags * mr_filt * mr_part, axis=0)
    dz = jnp.stack([dq, dkv * v, dkv * k], axis=1)
    dz_tail = shifted(dz[: taps - 1], "ctx", -1)
    dz_ext = jnp.concatenate([dz, dz_tail], axis=0)
    dp = jnp.zeros_like(dz)
    shorts = []
    for s in range(taps):
        dp = dp + short_filt[None, :, s, :] * dz_ext[s : s + rows]
        shorts.append(jnp.sum(dz * p_ext[taps - 1 - s : taps - 1 - s + rows].astype(f32), axis=0))
    short_part = jnp.stack(shorts, axis=1)
    dpb = dp.astype(bf16)
    dp_all = lax.all_gather(jnp.transpose(dpb, (1, 0, 2)), "ctx", axis=1, tiled=True)
    du_part = jnp.einsum("tjc,jdc->td", dpb, w_in, preferred_element_type=f32)
    du_part, h_ids_all = lax.optimization_barrier((du_part, h_ids_all))
    dot_part = jnp.sum(du_part * gain_full[None, :] * x0_full, axis=1)
    dot_rows = as_rows(jnp.concatenate(split2(dot_part)), cw)
    n_dot = dot_rows.shape[0]
    du_send = jnp.concatenate(
        [
            du_part.astype(bf16).reshape(rows, n_dp, cw),
            jnp.broadcast_to(dot_rows[:, None, :], (n_dot, n_dp, cw)),
        ],
        axis=0,
    )
    du_recv = lax.all_to_all(du_send, "dp", 1, 1, tiled=True).astype(f32)
    du = jnp.sum(du_recv[:rows], axis=1)
    dot_recv = jnp.sum(du_recv[rows:], axis=1).reshape(-1)
    row_dot = (dot_recv[:rows] + dot_recv[rows : 2 * rows])[:, None] / width
    gain_part = jnp.sum(du * x0 * r, axis=0)
    dn = du * gain[None, :]
    dx0 = dout + r * (dn - x0 * r * r * row_dot)

    small = jnp.concatenate(
        [
            gain_part,
            short_part.reshape(-1),
            mr_part.reshape(-1),
            rate_part,
            tag_part.reshape(-1),
            loss_part[None],
        ]
    )
    n_small = small.shape[0]
    dlog_parts = split2(dlog.reshape(-1))
    tail = jnp.concatenate([small.astype(bf16)] + dlog_parts)
    final = jnp.concatenate(
        [dx0.astype(bf16), as_rows(tail, cw)],
        axis=0,
    )
    final_all = lax.all_to_all(
        jnp.broadcast_to(final[None], (n_ctx,) + final.shape), "ctx", 0, 0, tiled=True
    )
    dx0_all = final_all[:, :rows].reshape(seq, cw).astype(f32)
    tail_all = final_all[:, rows:].reshape(n_ctx, -1).astype(f32)
    small_tot = jnp.sum(tail_all[:, :n_small], axis=0)
    n_dlog = rows * n_tags
    dlog_all = (
        tail_all[:, n_small : n_small + n_dlog] + tail_all[:, n_small + n_dlog : n_small + 2 * n_dlog]
    ).reshape(seq, n_tags)

    h_all = h_ids_all[:, :rows].reshape(seq, cw)
    id_rows = h_ids_all[:, rows:].reshape(n_ctx, -1).astype(jnp.int32)
    ids_all = (id_rows[:, :rows] * 32 + id_rows[:, rows : 2 * rows]).reshape(seq)

    f_cols = width // n_ctx
    w_tag_cols = lax.dynamic_slice_in_dim(w_tag_full_t, k_ctx * f_cols, f_cols, 1)
    dy_all = jnp.dot(dlog_all, w_tag_cols, precision=high).astype(bf16)
    d_w_out = lax.dot_general(h_all, dy_all, (((0,), (0,)), ((), ())), preferred_element_type=f32)

    all_mask = ids_all[:, None] == vocab_ids[None, :]
    all_hot = all_mask.astype(bf16)
    r_all = jnp.sum(jnp.where(all_mask, r_vocab[None, :], 0.0), axis=1)[:, None]
    embed_k = lax.dynamic_slice_in_dim(embed_full, k_ctx * f_cols, f_cols, 1)
    gain_k = lax.dynamic_slice_in_dim(gain_full, k_ctx * f_cols, f_cols, 0)
    x0_k = jnp.dot(all_hot, embed_k, preferred_element_type=f32)
    u_k = (x0_k * r_all * gain_k[None, :]).astype(bf16)
    d_w_in = jnp.einsum("td,jtc->jdc", u_k, dp_all, preferred_element_type=f32)

    v_rows = vocab // n_ctx
    own_hot = (ids_all[:, None] == (k_ctx * v_rows + jnp.arange(v_rows))[None, :]).astype(f32)
    d_embed = jnp.dot(own_hot.T, dx0_all, precision=high)

    pos = 0
    outs = []
    for size, shape in (
        (cw, (cw,)),
        (3 * taps * cw, (3, taps, cw)),
        (span * cw, (span, cw)),
        (cw, (cw,)),
        (cw * n_tags, (cw, n_tags)),
        (1, ()),
    ):
        outs.append(small_tot[pos : pos + size].reshape(shape))
        pos += size
    gain_tot, short_tot, mr_tot, rate_tot, tag_tot, loss_tot = outs
    loss = loss_tot / seq
    return (
        loss,
        block_out,
        d_embed,
        gain_tot,
        d_w_in,
        short_tot,
        mr_tot,
        rate_tot,
        d_w_out,
        tag_tot,
    )


def solution(mesh):
    placed = (
        P("ctx"),
        P("ctx"),
        P(None, "dp"),
        P("dp"),
        P(None, None, "dp"),
        P(None, None, "dp"),
        P(None, "dp"),
        P("dp"),
        P("dp", None),
        P("dp", None),
    )
    return jax.shard_map(
        block,
        mesh=mesh,
        in_specs=placed,
        out_specs=(
            P(),
            P("ctx", "dp"),
            P("ctx", "dp"),
            P("dp"),
            P(None, "ctx", "dp"),
            P(None, None, "dp"),
            P(None, "dp"),
            P("dp"),
            P("dp", "ctx"),
            P("dp", None),
        ),
        check_vma=False,
    )
```

```python
import jax
import jax.numpy as jnp
from jax import lax
from jax.sharding import PartitionSpec as P
from jax.experimental import pallas as pl

LANES = 128
ROW_BLOCK = 64


def medium_forward(kv_ext, taps_eff, rows):
    span, width = taps_eff.shape

    def kernel(kv_ref, g_ref, m_ref):
        for rb in range(0, rows, ROW_BLOCK):
            acc = jnp.zeros((ROW_BLOCK, LANES), jnp.float32)
            for s in range(span):
                start = span - 1 - s + rb
                acc = acc + g_ref[s : s + 1, :] * kv_ref[start : start + ROW_BLOCK, :]
            m_ref[rb : rb + ROW_BLOCK, :] = acc

    ext = kv_ext.shape[0]
    return pl.pallas_call(
        kernel,
        out_shape=jax.ShapeDtypeStruct((rows, width), jnp.float32),
        grid=(width // LANES,),
        in_specs=[
            pl.BlockSpec((ext, LANES), lambda c: (0, c)),
            pl.BlockSpec((span, LANES), lambda c: (0, c)),
        ],
        out_specs=pl.BlockSpec((rows, LANES), lambda c: (0, c)),
    )(kv_ext, taps_eff)


def medium_backward(dm_ext, kv_ext, taps_eff, rows):
    span, width = taps_eff.shape

    def kernel(dm_ref, kv_ref, g_ref, dkv_ref, corr_ref):
        for rb in range(0, rows, ROW_BLOCK):
            acc = jnp.zeros((ROW_BLOCK, LANES), jnp.float32)
            for s in range(span):
                acc = acc + g_ref[s : s + 1, :] * dm_ref[s + rb : s + rb + ROW_BLOCK, :]
            dkv_ref[rb : rb + ROW_BLOCK, :] = acc
        for s0 in range(0, span, 8):
            parts = []
            for s in range(s0, s0 + 8):
                start = span - 1 - s
                part = jnp.zeros((8, LANES), jnp.float32)
                for rb in range(0, rows, 8):
                    part = part + dm_ref[rb : rb + 8, :] * kv_ref[start + rb : start + rb + 8, :]
                parts.append(jnp.sum(part, axis=0, keepdims=True))
            corr_ref[s0 : s0 + 8, :] = jnp.concatenate(parts, axis=0)

    ext = kv_ext.shape[0]
    return pl.pallas_call(
        kernel,
        out_shape=(
            jax.ShapeDtypeStruct((rows, width), jnp.float32),
            jax.ShapeDtypeStruct((span, width), jnp.float32),
        ),
        grid=(width // LANES,),
        in_specs=[
            pl.BlockSpec((dm_ext.shape[0], LANES), lambda c: (0, c)),
            pl.BlockSpec((ext, LANES), lambda c: (0, c)),
            pl.BlockSpec((span, LANES), lambda c: (0, c)),
        ],
        out_specs=(
            pl.BlockSpec((rows, LANES), lambda c: (0, c)),
            pl.BlockSpec((span, LANES), lambda c: (0, c)),
        ),
    )(dm_ext, kv_ext, taps_eff)


def shifted(block, axis, distance):
    devices = range(lax.axis_size(axis))
    route = [(i - distance, i) for i in devices if i - distance in devices]
    return lax.ppermute(block, axis, route)


def short_filter(padded, filters, count):
    taps = filters.shape[1]
    total = jnp.zeros((count,) + padded.shape[1:], jnp.float32)
    for s in range(taps):
        total = total + filters[None, :, s, :] * padded[taps - 1 - s : taps - 1 - s + count].astype(
            jnp.float32
        )
    return total


def split3(x):
    parts = []
    rest = x
    for _ in range(3):
        part = lax.reduce_precision(rest, exponent_bits=8, mantissa_bits=7)
        parts.append(part)
        rest = rest - part
    return [p.astype(jnp.bfloat16) for p in parts]


def split2(x):
    hi = lax.reduce_precision(x, exponent_bits=8, mantissa_bits=7)
    return [hi.astype(jnp.bfloat16), (x - hi).astype(jnp.bfloat16)]


def as_rows(flat, width):
    pad = (-flat.shape[0]) % width
    return jnp.pad(flat, (0, pad)).reshape(-1, width)


def block(ids, tags, embed, gain, w_in, short_filt, mr_filt, rates, w_out, w_tag):
    f32 = jnp.float32
    bf16 = jnp.bfloat16
    high = lax.Precision.HIGHEST
    rows = ids.shape[0]
    vocab = embed.shape[0]
    cw = embed.shape[1]
    width = w_in.shape[1]
    taps = short_filt.shape[1]
    span = mr_filt.shape[0]
    n_tags = w_tag.shape[1]
    n_ctx = lax.axis_size("ctx")
    k_ctx = lax.axis_index("ctx")
    seq = rows * n_ctx

    n_dp = lax.axis_size("dp")
    half = vocab // 2
    packed = jnp.concatenate([embed[:half], jnp.stack(split3(gain), axis=0), w_tag.T], axis=0)
    packed_full = lax.all_gather(packed, "dp", axis=1, tiled=True)
    upper = lax.all_to_all(
        jnp.broadcast_to(embed[None, half:], (n_dp, vocab - half, cw)), "dp", 0, 0, tiled=True
    )
    upper_full = jnp.transpose(upper, (1, 0, 2)).reshape(vocab - half, width)
    w_out_later, upper_full = lax.optimization_barrier((w_out, upper_full))
    w_out_cols = lax.all_to_all(w_out_later, "dp", 1, 0, tiled=True)
    embed_full = jnp.concatenate([packed_full[:half], upper_full], axis=0)
    gain_full = (
        packed_full[half].astype(f32) + packed_full[half + 1].astype(f32)
    ) + packed_full[half + 2].astype(f32)
    w_tag_full_t = packed_full[half + 3 : half + 3 + n_tags].astype(f32)

    emb32 = embed_full.astype(f32)
    r_vocab = lax.rsqrt(jnp.sum(emb32 * emb32, axis=1) / width + 1e-06)
    vocab_ids = jnp.arange(vocab)
    id_mask = ids[:, None] == vocab_ids[None, :]
    id_hot = id_mask.astype(bf16)
    r = jnp.sum(jnp.where(id_mask, r_vocab[None, :], 0.0), axis=1)[:, None]
    x0_full = jnp.dot(id_hot, embed_full, preferred_element_type=f32)
    x0 = jnp.dot(id_hot, embed, preferred_element_type=f32)
    u = (x0_full * r * gain_full[None, :]).astype(bf16)
    proj = jnp.einsum("td,jdc->tjc", u, w_in, preferred_element_type=f32).astype(bf16)
    head = shifted(proj[rows - (taps - 1) :], "ctx", 1)
    p_ext = jnp.concatenate([head, proj], axis=0)
    z = short_filter(p_ext, short_filt, rows)
    kv = (z[:, 1] * z[:, 2]).astype(bf16)
    kv_head = shifted(kv[rows - (span - 1) :], "ctx", 1)
    kv_ext = jnp.concatenate([kv_head, kv, jnp.zeros((1,) + kv.shape[1:], kv.dtype)], axis=0)
    q = z[:, 0]
    k = z[:, 1]
    v = z[:, 2]
    lags = jnp.arange(span).astype(f32)[:, None]
    decay = jnp.exp(-rates[None, :] * lags)
    taps_eff = mr_filt * decay
    kv_wide = kv_ext.astype(f32)
    m = medium_forward(kv_wide, taps_eff, rows)
    h = (q * m).astype(bf16)
    h_full = lax.all_gather(h, "dp", axis=1, tiled=True)
    y = jnp.dot(h_full, w_out_cols, preferred_element_type=f32)
    block_out = (x0 + y).astype(bf16)
    id_hi = (ids // 32).astype(bf16)
    id_lo = (ids % 32).astype(bf16)
    h_ids = jnp.concatenate([h, as_rows(jnp.concatenate([id_hi, id_lo]), cw)], axis=0)
    h_ids_all = lax.all_gather(h_ids, "ctx", axis=0, tiled=True).reshape(n_ctx, -1, cw)
    logit_part = jnp.dot(block_out, w_tag, preferred_element_type=f32)
    logit_parts = lax.all_to_all(
        jnp.broadcast_to(logit_part[None], (n_dp,) + logit_part.shape), "dp", 0, 0, tiled=True
    )
    logits = jnp.sum(logit_parts, axis=0)
    top = jnp.max(logits, axis=1)
    lse = top + jnp.log(jnp.sum(jnp.exp(logits - top[:, None]), axis=1))
    tag_hot = (tags[:, None] == jnp.arange(n_tags)[None, :]).astype(f32)
    loss_part = jnp.sum(lse - jnp.sum(logits * tag_hot, axis=1))
    dlog = jnp.exp(logits - lse[:, None]) - tag_hot
    dout = jnp.dot(dlog, w_tag.astype(f32).T, precision=high)
    tag_part = jnp.dot(block_out.astype(f32).T, dlog, precision=high)
    dy_full = jnp.dot(dlog, w_tag_full_t, precision=high).astype(bf16)
    dh = lax.dot_general(dy_full, w_out, (((1,), (1,)), ((), ())), preferred_element_type=f32)
    dq = dh * m
    dm = dh * q
    dm_tail = shifted(dm[: span - 1].astype(bf16), "ctx", -1).astype(f32)
    dm_ext = jnp.concatenate([dm, dm_tail, jnp.zeros((1,) + dm.shape[1:], f32)], axis=0)
    dkv, corr = medium_backward(dm_ext, kv_wide, taps_eff, rows)
    mr_part = corr * decay
    rate_part = -jnp.sum(lags * mr_filt * mr_part, axis=0)
    dz = jnp.stack([dq, dkv * v, dkv * k], axis=1)
    dz_tail = shifted(dz[: taps - 1], "ctx", -1)
    dz_ext = jnp.concatenate([dz, dz_tail], axis=0)
    dp = jnp.zeros_like(dz)
    shorts = []
    for s in range(taps):
        dp = dp + short_filt[None, :, s, :] * dz_ext[s : s + rows]
        shorts.append(jnp.sum(dz * p_ext[taps - 1 - s : taps - 1 - s + rows].astype(f32), axis=0))
    short_part = jnp.stack(shorts, axis=1)
    dpb = dp.astype(bf16)
    dp01_all = lax.all_gather(
        jnp.transpose(dpb[:, :2], (1, 0, 2)), "ctx", axis=1, tiled=True
    )
    du_part = jnp.einsum("tjc,jdc->td", dpb, w_in, preferred_element_type=f32)
    du_part, h_ids_all = lax.optimization_barrier((du_part, h_ids_all))
    dot_part = jnp.sum(du_part * gain_full[None, :] * x0_full, axis=1)
    dot_rows = as_rows(jnp.concatenate(split2(dot_part)), cw)
    n_dot = dot_rows.shape[0]
    du_send = jnp.concatenate(
        [
            du_part.astype(bf16).reshape(rows, n_dp, cw),
            jnp.broadcast_to(dot_rows[:, None, :], (n_dot, n_dp, cw)),
        ],
        axis=0,
    )
    du_recv = lax.all_to_all(du_send, "dp", 1, 1, tiled=True).astype(f32)
    du = jnp.sum(du_recv[:rows], axis=1)
    dot_recv = jnp.sum(du_recv[rows:], axis=1).reshape(-1)
    row_dot = (dot_recv[:rows] + dot_recv[rows : 2 * rows])[:, None] / width
    gain_part = jnp.sum(du * x0 * r, axis=0)
    dn = du * gain[None, :]
    dx0 = dout + r * (dn - x0 * r * r * row_dot)

    small = jnp.concatenate(
        [
            gain_part,
            short_part.reshape(-1),
            mr_part.reshape(-1),
            rate_part,
            tag_part.reshape(-1),
            loss_part[None],
        ]
    )
    n_small = small.shape[0]
    dlog_parts = split2(dlog.reshape(-1))
    tail = jnp.concatenate([small.astype(bf16)] + dlog_parts)
    v_rows = vocab // n_ctx
    embed_part = jnp.dot(id_hot.astype(f32).T, dx0, precision=high)
    common = jnp.concatenate([dpb[:, 2], as_rows(tail, cw)], axis=0)
    final = jnp.concatenate(
        [
            embed_part.astype(bf16).reshape(n_ctx, v_rows, cw),
            jnp.broadcast_to(common[None], (n_ctx,) + common.shape),
        ],
        axis=1,
    )
    final_all = lax.all_to_all(final, "ctx", 0, 0, tiled=True)
    d_embed = jnp.sum(final_all[:, :v_rows].astype(f32), axis=0)
    dp2_all = final_all[:, v_rows : v_rows + rows].reshape(seq, cw)
    dp_all = jnp.concatenate([dp01_all, dp2_all[None]], axis=0)
    tail_all = final_all[:, v_rows + rows :].reshape(n_ctx, -1).astype(f32)
    small_tot = jnp.sum(tail_all[:, :n_small], axis=0)
    n_dlog = rows * n_tags
    dlog_all = (
        tail_all[:, n_small : n_small + n_dlog] + tail_all[:, n_small + n_dlog : n_small + 2 * n_dlog]
    ).reshape(seq, n_tags)

    h_all = h_ids_all[:, :rows].reshape(seq, cw)
    id_rows = h_ids_all[:, rows:].reshape(n_ctx, -1).astype(jnp.int32)
    ids_all = (id_rows[:, :rows] * 32 + id_rows[:, rows : 2 * rows]).reshape(seq)

    f_cols = width // n_ctx
    w_tag_cols = lax.dynamic_slice_in_dim(w_tag_full_t, k_ctx * f_cols, f_cols, 1)
    dy_all = jnp.dot(dlog_all, w_tag_cols, precision=high).astype(bf16)
    d_w_out = lax.dot_general(h_all, dy_all, (((0,), (0,)), ((), ())), preferred_element_type=f32)

    all_mask = ids_all[:, None] == vocab_ids[None, :]
    all_hot = all_mask.astype(bf16)
    r_all = jnp.sum(jnp.where(all_mask, r_vocab[None, :], 0.0), axis=1)[:, None]
    embed_k = lax.dynamic_slice_in_dim(embed_full, k_ctx * f_cols, f_cols, 1)
    gain_k = lax.dynamic_slice_in_dim(gain_full, k_ctx * f_cols, f_cols, 0)
    x0_k = jnp.dot(all_hot, embed_k, preferred_element_type=f32)
    u_k = (x0_k * r_all * gain_k[None, :]).astype(bf16)
    d_w_in = jnp.einsum("td,jtc->jdc", u_k, dp_all, preferred_element_type=f32)


    pos = 0
    outs = []
    for size, shape in (
        (cw, (cw,)),
        (3 * taps * cw, (3, taps, cw)),
        (span * cw, (span, cw)),
        (cw, (cw,)),
        (cw * n_tags, (cw, n_tags)),
        (1, ()),
    ):
        outs.append(small_tot[pos : pos + size].reshape(shape))
        pos += size
    gain_tot, short_tot, mr_tot, rate_tot, tag_tot, loss_tot = outs
    loss = loss_tot / seq
    return (
        loss,
        block_out,
        d_embed,
        gain_tot,
        d_w_in,
        short_tot,
        mr_tot,
        rate_tot,
        d_w_out,
        tag_tot,
    )


def solution(mesh):
    placed = (
        P("ctx"),
        P("ctx"),
        P(None, "dp"),
        P("dp"),
        P(None, None, "dp"),
        P(None, None, "dp"),
        P(None, "dp"),
        P("dp"),
        P("dp", None),
        P("dp", None),
    )
    return jax.shard_map(
        block,
        mesh=mesh,
        in_specs=placed,
        out_specs=(
            P(),
            P("ctx", "dp"),
            P("ctx", "dp"),
            P("dp"),
            P(None, "ctx", "dp"),
            P(None, None, "dp"),
            P(None, "dp"),
            P("dp"),
            P("dp", "ctx"),
            P("dp", None),
        ),
        check_vma=False,
    )
```

```python
import jax
import jax.numpy as jnp
from jax import lax
from jax.sharding import PartitionSpec as P
from jax.experimental import pallas as pl

LANES = 128
ROW_BLOCK = 64


def medium_forward(kv_ext, taps_eff, rows):
    span, width = taps_eff.shape

    def kernel(kv_ref, g_ref, m_ref):
        for rb in range(0, rows, ROW_BLOCK):

            def step(s, acc):
                start = span - 1 - s + rb
                return acc + g_ref[pl.ds(s, 1), :] * kv_ref[pl.ds(start, ROW_BLOCK), :]

            acc = lax.fori_loop(
                0, span, step, jnp.zeros((ROW_BLOCK, LANES), jnp.float32), unroll=8
            )
            m_ref[rb : rb + ROW_BLOCK, :] = acc

    ext = kv_ext.shape[0]
    return pl.pallas_call(
        kernel,
        out_shape=jax.ShapeDtypeStruct((rows, width), jnp.float32),
        grid=(width // LANES,),
        in_specs=[
            pl.BlockSpec((ext, LANES), lambda c: (0, c)),
            pl.BlockSpec((span, LANES), lambda c: (0, c)),
        ],
        out_specs=pl.BlockSpec((rows, LANES), lambda c: (0, c)),
    )(kv_ext, taps_eff)


def medium_backward(dm_ext, kv_ext, taps_eff, rows):
    span, width = taps_eff.shape

    def kernel(dm_ref, kv_ref, g_ref, dkv_ref, corr_ref):
        for rb in range(0, rows, ROW_BLOCK):

            def step(s, acc):
                return acc + g_ref[pl.ds(s, 1), :] * dm_ref[pl.ds(s + rb, ROW_BLOCK), :]

            acc = lax.fori_loop(
                0, span, step, jnp.zeros((ROW_BLOCK, LANES), jnp.float32), unroll=8
            )
            dkv_ref[rb : rb + ROW_BLOCK, :] = acc

        def lag_group(g, carry):
            s0 = pl.multiple_of(g * 8, 8)
            parts = []
            for i in range(8):
                start = span - 1 - s0 - i
                part = jnp.zeros((8, LANES), jnp.float32)
                for rb in range(0, rows, 8):
                    part = part + dm_ref[rb : rb + 8, :] * kv_ref[pl.ds(start + rb, 8), :]
                parts.append(jnp.sum(part, axis=0, keepdims=True))
            corr_ref[pl.ds(s0, 8), :] = jnp.concatenate(parts, axis=0)
            return carry

        lax.fori_loop(0, span // 8, lag_group, 0)

    ext = kv_ext.shape[0]
    return pl.pallas_call(
        kernel,
        out_shape=(
            jax.ShapeDtypeStruct((rows, width), jnp.float32),
            jax.ShapeDtypeStruct((span, width), jnp.float32),
        ),
        grid=(width // LANES,),
        in_specs=[
            pl.BlockSpec((dm_ext.shape[0], LANES), lambda c: (0, c)),
            pl.BlockSpec((ext, LANES), lambda c: (0, c)),
            pl.BlockSpec((span, LANES), lambda c: (0, c)),
        ],
        out_specs=(
            pl.BlockSpec((rows, LANES), lambda c: (0, c)),
            pl.BlockSpec((span, LANES), lambda c: (0, c)),
        ),
    )(dm_ext, kv_ext, taps_eff)


def shifted(block, axis, distance):
    devices = range(lax.axis_size(axis))
    route = [(i - distance, i) for i in devices if i - distance in devices]
    return lax.ppermute(block, axis, route)


def short_filter(padded, filters, count):
    taps = filters.shape[1]
    total = jnp.zeros((count,) + padded.shape[1:], jnp.float32)
    for s in range(taps):
        total = total + filters[None, :, s, :] * padded[taps - 1 - s : taps - 1 - s + count].astype(
            jnp.float32
        )
    return total


def split3(x):
    parts = []
    rest = x
    for _ in range(3):
        part = lax.reduce_precision(rest, exponent_bits=8, mantissa_bits=7)
        parts.append(part)
        rest = rest - part
    return [p.astype(jnp.bfloat16) for p in parts]


def split2(x):
    hi = lax.reduce_precision(x, exponent_bits=8, mantissa_bits=7)
    return [hi.astype(jnp.bfloat16), (x - hi).astype(jnp.bfloat16)]


def as_rows(flat, width):
    pad = (-flat.shape[0]) % width
    return jnp.pad(flat, (0, pad)).reshape(-1, width)


def block(ids, tags, embed, gain, w_in, short_filt, mr_filt, rates, w_out, w_tag):
    f32 = jnp.float32
    bf16 = jnp.bfloat16
    high = lax.Precision.HIGHEST
    rows = ids.shape[0]
    vocab = embed.shape[0]
    cw = embed.shape[1]
    width = w_in.shape[1]
    taps = short_filt.shape[1]
    span = mr_filt.shape[0]
    n_tags = w_tag.shape[1]
    n_ctx = lax.axis_size("ctx")
    k_ctx = lax.axis_index("ctx")
    seq = rows * n_ctx

    n_dp = lax.axis_size("dp")
    half = vocab // 2
    packed = jnp.concatenate([embed[:half], jnp.stack(split3(gain), axis=0), w_tag.T], axis=0)
    packed_full = lax.all_gather(packed, "dp", axis=1, tiled=True)
    upper = lax.all_to_all(
        jnp.broadcast_to(embed[None, half:], (n_dp, vocab - half, cw)), "dp", 0, 0, tiled=True
    )
    upper_full = jnp.transpose(upper, (1, 0, 2)).reshape(vocab - half, width)
    w_out_later, upper_full = lax.optimization_barrier((w_out, upper_full))
    w_out_cols = lax.all_to_all(w_out_later, "dp", 1, 0, tiled=True)
    embed_full = jnp.concatenate([packed_full[:half], upper_full], axis=0)
    gain_full = (
        packed_full[half].astype(f32) + packed_full[half + 1].astype(f32)
    ) + packed_full[half + 2].astype(f32)
    w_tag_full_t = packed_full[half + 3 : half + 3 + n_tags].astype(f32)

    emb32 = embed_full.astype(f32)
    r_vocab = lax.rsqrt(jnp.sum(emb32 * emb32, axis=1) / width + 1e-06)
    vocab_ids = jnp.arange(vocab)
    id_mask = ids[:, None] == vocab_ids[None, :]
    id_hot = id_mask.astype(bf16)
    r = jnp.sum(jnp.where(id_mask, r_vocab[None, :], 0.0), axis=1)[:, None]
    x0_full = jnp.dot(id_hot, embed_full, preferred_element_type=f32)
    x0 = jnp.dot(id_hot, embed, preferred_element_type=f32)
    u = (x0_full * r * gain_full[None, :]).astype(bf16)
    proj = jnp.einsum("td,jdc->tjc", u, w_in, preferred_element_type=f32).astype(bf16)
    head = shifted(proj[rows - (taps - 1) :], "ctx", 1)
    p_ext = jnp.concatenate([head, proj], axis=0)
    z = short_filter(p_ext, short_filt, rows)
    kv = (z[:, 1] * z[:, 2]).astype(bf16)
    kv_head = shifted(kv[rows - (span - 1) :], "ctx", 1)
    kv_ext = jnp.concatenate([kv_head, kv, jnp.zeros((1,) + kv.shape[1:], kv.dtype)], axis=0)
    q = z[:, 0]
    k = z[:, 1]
    v = z[:, 2]
    lags = jnp.arange(span).astype(f32)[:, None]
    decay = jnp.exp(-rates[None, :] * lags)
    taps_eff = mr_filt * decay
    kv_wide = kv_ext.astype(f32)
    m = medium_forward(kv_wide, taps_eff, rows)
    h = (q * m).astype(bf16)
    h_full = lax.all_gather(h, "dp", axis=1, tiled=True)
    y = jnp.dot(h_full, w_out_cols, preferred_element_type=f32)
    block_out = (x0 + y).astype(bf16)
    id_hi = (ids // 32).astype(bf16)
    id_lo = (ids % 32).astype(bf16)
    h_ids = jnp.concatenate([h, as_rows(jnp.concatenate([id_hi, id_lo]), cw)], axis=0)
    h_ids_all = lax.all_to_all(
        jnp.broadcast_to(h_ids[None], (n_ctx,) + h_ids.shape), "ctx", 0, 0, tiled=True
    )
    logit_part = jnp.dot(block_out, w_tag, preferred_element_type=f32)
    logit_parts = lax.all_to_all(
        jnp.broadcast_to(logit_part[None], (n_dp,) + logit_part.shape), "dp", 0, 0, tiled=True
    )
    logits = jnp.sum(logit_parts, axis=0)
    top = jnp.max(logits, axis=1)
    lse = top + jnp.log(jnp.sum(jnp.exp(logits - top[:, None]), axis=1))
    tag_hot = (tags[:, None] == jnp.arange(n_tags)[None, :]).astype(f32)
    loss_part = jnp.sum(lse - jnp.sum(logits * tag_hot, axis=1))
    dlog = jnp.exp(logits - lse[:, None]) - tag_hot
    dout = jnp.dot(dlog, w_tag.astype(f32).T, precision=high)
    tag_part = jnp.dot(block_out.astype(f32).T, dlog, precision=high)
    dy_full = jnp.dot(dlog, w_tag_full_t, precision=high).astype(bf16)
    dh = lax.dot_general(dy_full, w_out, (((1,), (1,)), ((), ())), preferred_element_type=f32)
    dq = dh * m
    dm = dh * q
    dm_tail = shifted(dm[: span - 1].astype(bf16), "ctx", -1).astype(f32)
    dm_ext = jnp.concatenate([dm, dm_tail, jnp.zeros((1,) + dm.shape[1:], f32)], axis=0)
    dkv, corr = medium_backward(dm_ext, kv_wide, taps_eff, rows)
    mr_part = corr * decay
    rate_part = -jnp.sum(lags * mr_filt * mr_part, axis=0)
    dz = jnp.stack([dq, dkv * v, dkv * k], axis=1)
    dz_tail = shifted(dz[: taps - 1], "ctx", -1)
    dz_ext = jnp.concatenate([dz, dz_tail], axis=0)
    dp = jnp.zeros_like(dz)
    shorts = []
    for s in range(taps):
        dp = dp + short_filt[None, :, s, :] * dz_ext[s : s + rows]
        shorts.append(jnp.sum(dz * p_ext[taps - 1 - s : taps - 1 - s + rows].astype(f32), axis=0))
    short_part = jnp.stack(shorts, axis=1)
    dpb = dp.astype(bf16)
    dp_all = lax.all_gather(jnp.transpose(dpb, (1, 0, 2)), "ctx", axis=1, tiled=True)
    du_part = jnp.einsum("tjc,jdc->td", dpb, w_in, preferred_element_type=f32)
    du_part, h_ids_all = lax.optimization_barrier((du_part, h_ids_all))
    dot_part = jnp.sum(du_part * gain_full[None, :] * x0_full, axis=1)
    dot_rows = as_rows(jnp.concatenate(split2(dot_part)), cw)
    n_dot = dot_rows.shape[0]
    du_send = jnp.concatenate(
        [
            du_part.astype(bf16).reshape(rows, n_dp, cw),
            jnp.broadcast_to(dot_rows[:, None, :], (n_dot, n_dp, cw)),
        ],
        axis=0,
    )
    du_recv = lax.all_to_all(du_send, "dp", 1, 1, tiled=True).astype(f32)
    du = jnp.sum(du_recv[:rows], axis=1)
    dot_recv = jnp.sum(du_recv[rows:], axis=1).reshape(-1)
    row_dot = (dot_recv[:rows] + dot_recv[rows : 2 * rows])[:, None] / width
    gain_part = jnp.sum(du * x0 * r, axis=0)
    dn = du * gain[None, :]
    dx0 = dout + r * (dn - x0 * r * r * row_dot)

    small = jnp.concatenate(
        [
            gain_part,
            short_part.reshape(-1),
            mr_part.reshape(-1),
            rate_part,
            tag_part.reshape(-1),
            loss_part[None],
        ]
    )
    n_small = small.shape[0]
    dlog_parts = split2(dlog.reshape(-1))
    tail = jnp.concatenate([small.astype(bf16)] + dlog_parts)
    final = jnp.concatenate(
        [dx0.astype(bf16), as_rows(tail, cw)],
        axis=0,
    )
    final_all = lax.all_to_all(
        jnp.broadcast_to(final[None], (n_ctx,) + final.shape), "ctx", 0, 0, tiled=True
    )
    dx0_all = final_all[:, :rows].reshape(seq, cw).astype(f32)
    tail_all = final_all[:, rows:].reshape(n_ctx, -1).astype(f32)
    small_tot = jnp.sum(tail_all[:, :n_small], axis=0)
    n_dlog = rows * n_tags
    dlog_all = (
        tail_all[:, n_small : n_small + n_dlog] + tail_all[:, n_small + n_dlog : n_small + 2 * n_dlog]
    ).reshape(seq, n_tags)

    h_all = h_ids_all[:, :rows].reshape(seq, cw)
    id_rows = h_ids_all[:, rows:].reshape(n_ctx, -1).astype(jnp.int32)
    ids_all = (id_rows[:, :rows] * 32 + id_rows[:, rows : 2 * rows]).reshape(seq)

    f_cols = width // n_ctx
    w_tag_cols = lax.dynamic_slice_in_dim(w_tag_full_t, k_ctx * f_cols, f_cols, 1)
    dy_all = jnp.dot(dlog_all, w_tag_cols, precision=high).astype(bf16)
    d_w_out = lax.dot_general(h_all, dy_all, (((0,), (0,)), ((), ())), preferred_element_type=f32)

    all_mask = ids_all[:, None] == vocab_ids[None, :]
    all_hot = all_mask.astype(bf16)
    r_all = jnp.sum(jnp.where(all_mask, r_vocab[None, :], 0.0), axis=1)[:, None]
    embed_k = lax.dynamic_slice_in_dim(embed_full, k_ctx * f_cols, f_cols, 1)
    gain_k = lax.dynamic_slice_in_dim(gain_full, k_ctx * f_cols, f_cols, 0)
    x0_k = jnp.dot(all_hot, embed_k, preferred_element_type=f32)
    u_k = (x0_k * r_all * gain_k[None, :]).astype(bf16)
    d_w_in = jnp.einsum("td,jtc->jdc", u_k, dp_all, preferred_element_type=f32)

    v_rows = vocab // n_ctx
    own_hot = (ids_all[:, None] == (k_ctx * v_rows + jnp.arange(v_rows))[None, :]).astype(f32)
    d_embed = jnp.dot(own_hot.T, dx0_all, precision=high)

    pos = 0
    outs = []
    for size, shape in (
        (cw, (cw,)),
        (3 * taps * cw, (3, taps, cw)),
        (span * cw, (span, cw)),
        (cw, (cw,)),
        (cw * n_tags, (cw, n_tags)),
        (1, ()),
    ):
        outs.append(small_tot[pos : pos + size].reshape(shape))
        pos += size
    gain_tot, short_tot, mr_tot, rate_tot, tag_tot, loss_tot = outs
    loss = loss_tot / seq
    return (
        loss,
        block_out,
        d_embed,
        gain_tot,
        d_w_in,
        short_tot,
        mr_tot,
        rate_tot,
        d_w_out,
        tag_tot,
    )


def solution(mesh):
    placed = (
        P("ctx"),
        P("ctx"),
        P(None, "dp"),
        P("dp"),
        P(None, None, "dp"),
        P(None, None, "dp"),
        P(None, "dp"),
        P("dp"),
        P("dp", None),
        P("dp", None),
    )
    return jax.shard_map(
        block,
        mesh=mesh,
        in_specs=placed,
        out_specs=(
            P(),
            P("ctx", "dp"),
            P("ctx", "dp"),
            P("dp"),
            P(None, "ctx", "dp"),
            P(None, None, "dp"),
            P(None, "dp"),
            P("dp"),
            P("dp", "ctx"),
            P("dp", None),
        ),
        check_vma=False,
    )
```

```python
import jax
import jax.numpy as jnp
from jax import lax
from jax.sharding import PartitionSpec as P
from jax.experimental import pallas as pl

LANES = 128
ROW_BLOCK = 64


def medium_forward(kv_ext, taps_eff, rows):
    span, width = taps_eff.shape

    def kernel(kv_ref, g_ref, m_ref):
        for rb in range(0, rows, ROW_BLOCK):

            def step(s, acc):
                start = span - 1 - s + rb
                return acc + g_ref[pl.ds(s, 1), :] * kv_ref[pl.ds(start, ROW_BLOCK), :]

            acc = lax.fori_loop(
                0, span, step, jnp.zeros((ROW_BLOCK, LANES), jnp.float32), unroll=8
            )
            m_ref[rb : rb + ROW_BLOCK, :] = acc

    ext = kv_ext.shape[0]
    return pl.pallas_call(
        kernel,
        out_shape=jax.ShapeDtypeStruct((rows, width), jnp.float32),
        grid=(width // LANES,),
        in_specs=[
            pl.BlockSpec((ext, LANES), lambda c: (0, c)),
            pl.BlockSpec((span, LANES), lambda c: (0, c)),
        ],
        out_specs=pl.BlockSpec((rows, LANES), lambda c: (0, c)),
    )(kv_ext, taps_eff)


def medium_backward(dm_ext, kv_ext, taps_eff, rows):
    span, width = taps_eff.shape

    def kernel(dm_ref, kv_ref, g_ref, dkv_ref, corr_ref):
        for rb in range(0, rows, ROW_BLOCK):

            def step(s, acc):
                return acc + g_ref[pl.ds(s, 1), :] * dm_ref[pl.ds(s + rb, ROW_BLOCK), :]

            acc = lax.fori_loop(
                0, span, step, jnp.zeros((ROW_BLOCK, LANES), jnp.float32), unroll=8
            )
            dkv_ref[rb : rb + ROW_BLOCK, :] = acc

        for s0 in range(0, span, 8):
            parts = []
            for s in range(s0, s0 + 8):
                start = span - 1 - s
                part = jnp.zeros((8, LANES), jnp.float32)
                for rb in range(0, rows, 8):
                    part = part + dm_ref[rb : rb + 8, :] * kv_ref[start + rb : start + rb + 8, :]
                parts.append(jnp.sum(part, axis=0, keepdims=True))
            corr_ref[s0 : s0 + 8, :] = jnp.concatenate(parts, axis=0)

    ext = kv_ext.shape[0]
    return pl.pallas_call(
        kernel,
        out_shape=(
            jax.ShapeDtypeStruct((rows, width), jnp.float32),
            jax.ShapeDtypeStruct((span, width), jnp.float32),
        ),
        grid=(width // LANES,),
        in_specs=[
            pl.BlockSpec((dm_ext.shape[0], LANES), lambda c: (0, c)),
            pl.BlockSpec((ext, LANES), lambda c: (0, c)),
            pl.BlockSpec((span, LANES), lambda c: (0, c)),
        ],
        out_specs=(
            pl.BlockSpec((rows, LANES), lambda c: (0, c)),
            pl.BlockSpec((span, LANES), lambda c: (0, c)),
        ),
    )(dm_ext, kv_ext, taps_eff)


def shifted(block, axis, distance):
    devices = range(lax.axis_size(axis))
    route = [(i - distance, i) for i in devices if i - distance in devices]
    return lax.ppermute(block, axis, route)


def short_filter(padded, filters, count):
    taps = filters.shape[1]
    total = jnp.zeros((count,) + padded.shape[1:], jnp.float32)
    for s in range(taps):
        total = total + filters[None, :, s, :] * padded[taps - 1 - s : taps - 1 - s + count].astype(
            jnp.float32
        )
    return total


def split3(x):
    parts = []
    rest = x
    for _ in range(3):
        part = lax.reduce_precision(rest, exponent_bits=8, mantissa_bits=7)
        parts.append(part)
        rest = rest - part
    return [p.astype(jnp.bfloat16) for p in parts]


def split2(x):
    hi = lax.reduce_precision(x, exponent_bits=8, mantissa_bits=7)
    return [hi.astype(jnp.bfloat16), (x - hi).astype(jnp.bfloat16)]


def as_rows(flat, width):
    pad = (-flat.shape[0]) % width
    return jnp.pad(flat, (0, pad)).reshape(-1, width)


def block(ids, tags, embed, gain, w_in, short_filt, mr_filt, rates, w_out, w_tag):
    f32 = jnp.float32
    bf16 = jnp.bfloat16
    high = lax.Precision.HIGHEST
    rows = ids.shape[0]
    vocab = embed.shape[0]
    cw = embed.shape[1]
    width = w_in.shape[1]
    taps = short_filt.shape[1]
    span = mr_filt.shape[0]
    n_tags = w_tag.shape[1]
    n_ctx = lax.axis_size("ctx")
    k_ctx = lax.axis_index("ctx")
    seq = rows * n_ctx

    n_dp = lax.axis_size("dp")
    half = vocab // 2
    packed = jnp.concatenate([embed[:half], jnp.stack(split3(gain), axis=0), w_tag.T], axis=0)
    packed_full = lax.all_gather(packed, "dp", axis=1, tiled=True)
    upper = lax.all_to_all(
        jnp.broadcast_to(embed[None, half:], (n_dp, vocab - half, cw)), "dp", 0, 0, tiled=True
    )
    upper_full = jnp.transpose(upper, (1, 0, 2)).reshape(vocab - half, width)
    w_out_later, upper_full = lax.optimization_barrier((w_out, upper_full))
    w_out_cols = lax.all_to_all(w_out_later, "dp", 1, 0, tiled=True)
    embed_full = jnp.concatenate([packed_full[:half], upper_full], axis=0)
    gain_full = (
        packed_full[half].astype(f32) + packed_full[half + 1].astype(f32)
    ) + packed_full[half + 2].astype(f32)
    w_tag_full_t = packed_full[half + 3 : half + 3 + n_tags].astype(f32)

    emb32 = embed_full.astype(f32)
    r_vocab = lax.rsqrt(jnp.sum(emb32 * emb32, axis=1) / width + 1e-06)
    vocab_ids = jnp.arange(vocab)
    id_mask = ids[:, None] == vocab_ids[None, :]
    id_hot = id_mask.astype(bf16)
    r = jnp.sum(jnp.where(id_mask, r_vocab[None, :], 0.0), axis=1)[:, None]
    x0_full = jnp.dot(id_hot, embed_full, preferred_element_type=f32)
    x0 = jnp.dot(id_hot, embed, preferred_element_type=f32)
    u = (x0_full * r * gain_full[None, :]).astype(bf16)
    proj = jnp.einsum("td,jdc->tjc", u, w_in, preferred_element_type=f32).astype(bf16)
    head = shifted(proj[rows - (taps - 1) :], "ctx", 1)
    p_ext = jnp.concatenate([head, proj], axis=0)
    z = short_filter(p_ext, short_filt, rows)
    kv = (z[:, 1] * z[:, 2]).astype(bf16)
    kv_head = shifted(kv[rows - (span - 1) :], "ctx", 1)
    kv_ext = jnp.concatenate([kv_head, kv, jnp.zeros((1,) + kv.shape[1:], kv.dtype)], axis=0)
    q = z[:, 0]
    k = z[:, 1]
    v = z[:, 2]
    lags = jnp.arange(span).astype(f32)[:, None]
    decay = jnp.exp(-rates[None, :] * lags)
    taps_eff = mr_filt * decay
    kv_wide = kv_ext.astype(f32)
    m = medium_forward(kv_wide, taps_eff, rows)
    h = (q * m).astype(bf16)
    h_full = lax.all_gather(h, "dp", axis=1, tiled=True)
    y = jnp.dot(h_full, w_out_cols, preferred_element_type=f32)
    block_out = (x0 + y).astype(bf16)
    id_hi = (ids // 32).astype(bf16)
    id_lo = (ids % 32).astype(bf16)
    h_ids = jnp.concatenate([h, as_rows(jnp.concatenate([id_hi, id_lo]), cw)], axis=0)
    h_ids_all = lax.all_to_all(
        jnp.broadcast_to(h_ids[None], (n_ctx,) + h_ids.shape), "ctx", 0, 0, tiled=True
    )
    logit_part = jnp.dot(block_out, w_tag, preferred_element_type=f32)
    logit_parts = lax.all_to_all(
        jnp.broadcast_to(logit_part[None], (n_dp,) + logit_part.shape), "dp", 0, 0, tiled=True
    )
    logits = jnp.sum(logit_parts, axis=0)
    top = jnp.max(logits, axis=1)
    lse = top + jnp.log(jnp.sum(jnp.exp(logits - top[:, None]), axis=1))
    tag_hot = (tags[:, None] == jnp.arange(n_tags)[None, :]).astype(f32)
    loss_part = jnp.sum(lse - jnp.sum(logits * tag_hot, axis=1))
    dlog = jnp.exp(logits - lse[:, None]) - tag_hot
    dout = jnp.dot(dlog, w_tag.astype(f32).T, precision=high)
    tag_part = jnp.dot(block_out.astype(f32).T, dlog, precision=high)
    dy_full = jnp.dot(dlog, w_tag_full_t, precision=high).astype(bf16)
    dh = lax.dot_general(dy_full, w_out, (((1,), (1,)), ((), ())), preferred_element_type=f32)
    dq = dh * m
    dm = dh * q
    dm_tail = shifted(dm[: span - 1].astype(bf16), "ctx", -1).astype(f32)
    dm_ext = jnp.concatenate([dm, dm_tail, jnp.zeros((1,) + dm.shape[1:], f32)], axis=0)
    dkv, corr = medium_backward(dm_ext, kv_wide, taps_eff, rows)
    mr_part = corr * decay
    rate_part = -jnp.sum(lags * mr_filt * mr_part, axis=0)
    dz = jnp.stack([dq, dkv * v, dkv * k], axis=1)
    dz_tail = shifted(dz[: taps - 1], "ctx", -1)
    dz_ext = jnp.concatenate([dz, dz_tail], axis=0)
    dp = jnp.zeros_like(dz)
    shorts = []
    for s in range(taps):
        dp = dp + short_filt[None, :, s, :] * dz_ext[s : s + rows]
        shorts.append(jnp.sum(dz * p_ext[taps - 1 - s : taps - 1 - s + rows].astype(f32), axis=0))
    short_part = jnp.stack(shorts, axis=1)
    dpb = dp.astype(bf16)
    dp_all = lax.all_gather(jnp.transpose(dpb, (1, 0, 2)), "ctx", axis=1, tiled=True)
    du_part = jnp.einsum("tjc,jdc->td", dpb, w_in, preferred_element_type=f32)
    du_part, h_ids_all = lax.optimization_barrier((du_part, h_ids_all))
    dot_part = jnp.sum(du_part * gain_full[None, :] * x0_full, axis=1)
    dot_rows = as_rows(jnp.concatenate(split2(dot_part)), cw)
    n_dot = dot_rows.shape[0]
    du_send = jnp.concatenate(
        [
            du_part.astype(bf16).reshape(rows, n_dp, cw),
            jnp.broadcast_to(dot_rows[:, None, :], (n_dot, n_dp, cw)),
        ],
        axis=0,
    )
    du_recv = lax.all_to_all(du_send, "dp", 1, 1, tiled=True).astype(f32)
    du = jnp.sum(du_recv[:rows], axis=1)
    dot_recv = jnp.sum(du_recv[rows:], axis=1).reshape(-1)
    row_dot = (dot_recv[:rows] + dot_recv[rows : 2 * rows])[:, None] / width
    gain_part = jnp.sum(du * x0 * r, axis=0)
    dn = du * gain[None, :]
    dx0 = dout + r * (dn - x0 * r * r * row_dot)

    small = jnp.concatenate(
        [
            gain_part,
            short_part.reshape(-1),
            mr_part.reshape(-1),
            rate_part,
            tag_part.reshape(-1),
            loss_part[None],
        ]
    )
    n_small = small.shape[0]
    dlog_parts = split2(dlog.reshape(-1))
    tail = jnp.concatenate([small.astype(bf16)] + dlog_parts)
    final = jnp.concatenate(
        [dx0.astype(bf16), as_rows(tail, cw)],
        axis=0,
    )
    final_all = lax.all_to_all(
        jnp.broadcast_to(final[None], (n_ctx,) + final.shape), "ctx", 0, 0, tiled=True
    )
    dx0_all = final_all[:, :rows].reshape(seq, cw).astype(f32)
    tail_all = final_all[:, rows:].reshape(n_ctx, -1).astype(f32)
    small_tot = jnp.sum(tail_all[:, :n_small], axis=0)
    n_dlog = rows * n_tags
    dlog_all = (
        tail_all[:, n_small : n_small + n_dlog] + tail_all[:, n_small + n_dlog : n_small + 2 * n_dlog]
    ).reshape(seq, n_tags)

    h_all = h_ids_all[:, :rows].reshape(seq, cw)
    id_rows = h_ids_all[:, rows:].reshape(n_ctx, -1).astype(jnp.int32)
    ids_all = (id_rows[:, :rows] * 32 + id_rows[:, rows : 2 * rows]).reshape(seq)

    f_cols = width // n_ctx
    w_tag_cols = lax.dynamic_slice_in_dim(w_tag_full_t, k_ctx * f_cols, f_cols, 1)
    dy_all = jnp.dot(dlog_all, w_tag_cols, precision=high).astype(bf16)
    d_w_out = lax.dot_general(h_all, dy_all, (((0,), (0,)), ((), ())), preferred_element_type=f32)

    all_mask = ids_all[:, None] == vocab_ids[None, :]
    all_hot = all_mask.astype(bf16)
    r_all = jnp.sum(jnp.where(all_mask, r_vocab[None, :], 0.0), axis=1)[:, None]
    embed_k = lax.dynamic_slice_in_dim(embed_full, k_ctx * f_cols, f_cols, 1)
    gain_k = lax.dynamic_slice_in_dim(gain_full, k_ctx * f_cols, f_cols, 0)
    x0_k = jnp.dot(all_hot, embed_k, preferred_element_type=f32)
    u_k = (x0_k * r_all * gain_k[None, :]).astype(bf16)
    d_w_in = jnp.einsum("td,jtc->jdc", u_k, dp_all, preferred_element_type=f32)

    v_rows = vocab // n_ctx
    own_hot = (ids_all[:, None] == (k_ctx * v_rows + jnp.arange(v_rows))[None, :]).astype(f32)
    d_embed = jnp.dot(own_hot.T, dx0_all, precision=high)

    pos = 0
    outs = []
    for size, shape in (
        (cw, (cw,)),
        (3 * taps * cw, (3, taps, cw)),
        (span * cw, (span, cw)),
        (cw, (cw,)),
        (cw * n_tags, (cw, n_tags)),
        (1, ()),
    ):
        outs.append(small_tot[pos : pos + size].reshape(shape))
        pos += size
    gain_tot, short_tot, mr_tot, rate_tot, tag_tot, loss_tot = outs
    loss = loss_tot / seq
    return (
        loss,
        block_out,
        d_embed,
        gain_tot,
        d_w_in,
        short_tot,
        mr_tot,
        rate_tot,
        d_w_out,
        tag_tot,
    )


def solution(mesh):
    placed = (
        P("ctx"),
        P("ctx"),
        P(None, "dp"),
        P("dp"),
        P(None, None, "dp"),
        P(None, None, "dp"),
        P(None, "dp"),
        P("dp"),
        P("dp", None),
        P("dp", None),
    )
    return jax.shard_map(
        block,
        mesh=mesh,
        in_specs=placed,
        out_specs=(
            P(),
            P("ctx", "dp"),
            P("ctx", "dp"),
            P("dp"),
            P(None, "ctx", "dp"),
            P(None, None, "dp"),
            P(None, "dp"),
            P("dp"),
            P("dp", "ctx"),
            P("dp", None),
        ),
        check_vma=False,
    )
```

```python
import jax
import jax.numpy as jnp
from jax import lax
from jax.sharding import PartitionSpec as P
from jax.experimental import pallas as pl

LANES = 128
ROW_BLOCK = 64


def medium_forward(kv_ext, taps_eff, rows):
    span, width = taps_eff.shape

    def kernel(kv_ref, g_ref, m_ref):
        for rb in range(0, rows, ROW_BLOCK):

            def step(s, acc):
                start = span - 1 - s + rb
                return acc + g_ref[pl.ds(s, 1), :] * kv_ref[pl.ds(start, ROW_BLOCK), :]

            acc = lax.fori_loop(
                0, span, step, jnp.zeros((ROW_BLOCK, LANES), jnp.float32), unroll=8
            )
            m_ref[rb : rb + ROW_BLOCK, :] = acc

    ext = kv_ext.shape[0]
    return pl.pallas_call(
        kernel,
        out_shape=jax.ShapeDtypeStruct((rows, width), jnp.float32),
        grid=(width // LANES,),
        in_specs=[
            pl.BlockSpec((ext, LANES), lambda c: (0, c)),
            pl.BlockSpec((span, LANES), lambda c: (0, c)),
        ],
        out_specs=pl.BlockSpec((rows, LANES), lambda c: (0, c)),
    )(kv_ext, taps_eff)


def medium_backward(dm_ext, kv_ext, taps_eff, rows):
    span, width = taps_eff.shape

    def kernel(dm_ref, kv_ref, g_ref, dkv_ref, corr_ref):
        for rb in range(0, rows, ROW_BLOCK):

            def step(s, acc):
                return acc + g_ref[pl.ds(s, 1), :] * dm_ref[pl.ds(s + rb, ROW_BLOCK), :]

            acc = lax.fori_loop(
                0, span, step, jnp.zeros((ROW_BLOCK, LANES), jnp.float32), unroll=8
            )
            dkv_ref[rb : rb + ROW_BLOCK, :] = acc

        for s0 in range(0, span, 8):
            parts = []
            for s in range(s0, s0 + 8):
                start = span - 1 - s
                part = jnp.zeros((8, LANES), jnp.float32)
                for rb in range(0, rows, 8):
                    part = part + dm_ref[rb : rb + 8, :] * kv_ref[start + rb : start + rb + 8, :]
                parts.append(jnp.sum(part, axis=0, keepdims=True))
            corr_ref[s0 : s0 + 8, :] = jnp.concatenate(parts, axis=0)

    ext = kv_ext.shape[0]
    return pl.pallas_call(
        kernel,
        out_shape=(
            jax.ShapeDtypeStruct((rows, width), jnp.float32),
            jax.ShapeDtypeStruct((span, width), jnp.float32),
        ),
        grid=(width // LANES,),
        in_specs=[
            pl.BlockSpec((dm_ext.shape[0], LANES), lambda c: (0, c)),
            pl.BlockSpec((ext, LANES), lambda c: (0, c)),
            pl.BlockSpec((span, LANES), lambda c: (0, c)),
        ],
        out_specs=(
            pl.BlockSpec((rows, LANES), lambda c: (0, c)),
            pl.BlockSpec((span, LANES), lambda c: (0, c)),
        ),
    )(dm_ext, kv_ext, taps_eff)


def shifted(block, axis, distance):
    devices = range(lax.axis_size(axis))
    route = [(i - distance, i) for i in devices if i - distance in devices]
    return lax.ppermute(block, axis, route)


def short_filter(padded, filters, count):
    taps = filters.shape[1]
    total = jnp.zeros((count,) + padded.shape[1:], jnp.float32)
    for s in range(taps):
        total = total + filters[None, :, s, :] * padded[taps - 1 - s : taps - 1 - s + count].astype(
            jnp.float32
        )
    return total


def split3(x):
    parts = []
    rest = x
    for _ in range(3):
        part = lax.reduce_precision(rest, exponent_bits=8, mantissa_bits=7)
        parts.append(part)
        rest = rest - part
    return [p.astype(jnp.bfloat16) for p in parts]


def split2(x):
    hi = lax.reduce_precision(x, exponent_bits=8, mantissa_bits=7)
    return [hi.astype(jnp.bfloat16), (x - hi).astype(jnp.bfloat16)]


def as_rows(flat, width):
    pad = (-flat.shape[0]) % width
    return jnp.pad(flat, (0, pad)).reshape(-1, width)


def block(ids, tags, embed, gain, w_in, short_filt, mr_filt, rates, w_out, w_tag):
    f32 = jnp.float32
    bf16 = jnp.bfloat16
    high = lax.Precision.HIGHEST
    rows = ids.shape[0]
    vocab = embed.shape[0]
    cw = embed.shape[1]
    width = w_in.shape[1]
    taps = short_filt.shape[1]
    span = mr_filt.shape[0]
    n_tags = w_tag.shape[1]
    n_ctx = lax.axis_size("ctx")
    k_ctx = lax.axis_index("ctx")
    seq = rows * n_ctx

    n_dp = lax.axis_size("dp")
    half = vocab // 2
    packed = jnp.concatenate([embed[:half], jnp.stack(split3(gain), axis=0), w_tag.T], axis=0)
    packed_full = lax.all_gather(packed, "dp", axis=1, tiled=True)
    upper = lax.all_to_all(
        jnp.broadcast_to(embed[None, half:], (n_dp, vocab - half, cw)), "dp", 0, 0, tiled=True
    )
    upper_full = jnp.transpose(upper, (1, 0, 2)).reshape(vocab - half, width)
    w_out_later, upper_full = lax.optimization_barrier((w_out, upper_full))
    w_out_cols = lax.all_to_all(w_out_later, "dp", 1, 0, tiled=True)
    embed_full = jnp.concatenate([packed_full[:half], upper_full], axis=0)
    gain_full = (
        packed_full[half].astype(f32) + packed_full[half + 1].astype(f32)
    ) + packed_full[half + 2].astype(f32)
    w_tag_full_t = packed_full[half + 3 : half + 3 + n_tags].astype(f32)

    emb32 = embed_full.astype(f32)
    r_vocab = lax.rsqrt(jnp.sum(emb32 * emb32, axis=1) / width + 1e-06)
    vocab_ids = jnp.arange(vocab)
    id_mask = ids[:, None] == vocab_ids[None, :]
    id_hot = id_mask.astype(bf16)
    r = jnp.sum(jnp.where(id_mask, r_vocab[None, :], 0.0), axis=1)[:, None]
    x0_full = jnp.dot(id_hot, embed_full, preferred_element_type=f32)
    x0 = jnp.dot(id_hot, embed, preferred_element_type=f32)
    u = (x0_full * r * gain_full[None, :]).astype(bf16)
    proj = jnp.einsum("td,jdc->tjc", u, w_in, preferred_element_type=f32).astype(bf16)
    head = shifted(proj[rows - (taps - 1) :], "ctx", 1)
    p_ext = jnp.concatenate([head, proj], axis=0)
    z = short_filter(p_ext, short_filt, rows)
    kv = (z[:, 1] * z[:, 2]).astype(bf16)
    kv_head = shifted(kv[rows - (span - 1) :], "ctx", 1)
    kv_ext = jnp.concatenate([kv_head, kv, jnp.zeros((1,) + kv.shape[1:], kv.dtype)], axis=0)
    q = z[:, 0]
    k = z[:, 1]
    v = z[:, 2]
    lags = jnp.arange(span).astype(f32)[:, None]
    decay = jnp.exp(-rates[None, :] * lags)
    taps_eff = mr_filt * decay
    kv_wide = kv_ext.astype(f32)
    m = medium_forward(kv_wide, taps_eff, rows)
    h = (q * m).astype(bf16)
    h_full = lax.all_gather(h, "dp", axis=1, tiled=True)
    y = jnp.dot(h_full, w_out_cols, preferred_element_type=f32)
    block_out = (x0 + y).astype(bf16)
    id_hi = (ids // 32).astype(bf16)
    id_lo = (ids % 32).astype(bf16)
    logit_part = jnp.dot(block_out, w_tag, preferred_element_type=f32)
    logit_parts = lax.all_to_all(
        jnp.broadcast_to(logit_part[None], (n_dp,) + logit_part.shape), "dp", 0, 0, tiled=True
    )
    logits = jnp.sum(logit_parts, axis=0)
    top = jnp.max(logits, axis=1)
    lse = top + jnp.log(jnp.sum(jnp.exp(logits - top[:, None]), axis=1))
    tag_hot = (tags[:, None] == jnp.arange(n_tags)[None, :]).astype(f32)
    loss_part = jnp.sum(lse - jnp.sum(logits * tag_hot, axis=1))
    dlog = jnp.exp(logits - lse[:, None]) - tag_hot
    id_dlog = jnp.concatenate([id_hi, id_lo] + split2(dlog.reshape(-1)))
    h_ids = jnp.concatenate([h, as_rows(id_dlog, cw)], axis=0)
    h_ids_all = lax.all_to_all(
        jnp.broadcast_to(h_ids[None], (n_ctx,) + h_ids.shape), "ctx", 0, 0, tiled=True
    )
    dout = jnp.dot(dlog, w_tag.astype(f32).T, precision=high)
    tag_part = jnp.dot(block_out.astype(f32).T, dlog, precision=high)
    dy_full = jnp.dot(dlog, w_tag_full_t, precision=high).astype(bf16)
    dh = lax.dot_general(dy_full, w_out, (((1,), (1,)), ((), ())), preferred_element_type=f32)
    dq = dh * m
    dm = dh * q
    dm_tail = shifted(dm[: span - 1].astype(bf16), "ctx", -1).astype(f32)
    dm_ext = jnp.concatenate([dm, dm_tail, jnp.zeros((1,) + dm.shape[1:], f32)], axis=0)
    dkv, corr = medium_backward(dm_ext, kv_wide, taps_eff, rows)
    mr_part = corr * decay
    rate_part = -jnp.sum(lags * mr_filt * mr_part, axis=0)
    dz = jnp.stack([dq, dkv * v, dkv * k], axis=1)
    dz_tail = shifted(dz[: taps - 1], "ctx", -1)
    dz_ext = jnp.concatenate([dz, dz_tail], axis=0)
    dp = jnp.zeros_like(dz)
    shorts = []
    for s in range(taps):
        dp = dp + short_filt[None, :, s, :] * dz_ext[s : s + rows]
        shorts.append(jnp.sum(dz * p_ext[taps - 1 - s : taps - 1 - s + rows].astype(f32), axis=0))
    short_part = jnp.stack(shorts, axis=1)
    dpb = dp.astype(bf16)
    dp_all = lax.all_gather(jnp.transpose(dpb, (1, 0, 2)), "ctx", axis=1, tiled=True)
    du_part = jnp.einsum("tjc,jdc->td", dpb, w_in, preferred_element_type=f32)
    du_part, h_ids_all = lax.optimization_barrier((du_part, h_ids_all))
    dot_part = jnp.sum(du_part * gain_full[None, :] * x0_full, axis=1)
    dot_rows = as_rows(jnp.concatenate(split2(dot_part)), cw)
    n_dot = dot_rows.shape[0]
    du_send = jnp.concatenate(
        [
            du_part.astype(bf16).reshape(rows, n_dp, cw),
            jnp.broadcast_to(dot_rows[:, None, :], (n_dot, n_dp, cw)),
        ],
        axis=0,
    )
    du_recv = lax.all_to_all(du_send, "dp", 1, 1, tiled=True).astype(f32)
    du = jnp.sum(du_recv[:rows], axis=1)
    dot_recv = jnp.sum(du_recv[rows:], axis=1).reshape(-1)
    row_dot = (dot_recv[:rows] + dot_recv[rows : 2 * rows])[:, None] / width
    gain_part = jnp.sum(du * x0 * r, axis=0)
    dn = du * gain[None, :]
    dx0 = dout + r * (dn - x0 * r * r * row_dot)

    small = jnp.concatenate(
        [
            gain_part,
            short_part.reshape(-1),
            mr_part.reshape(-1),
            rate_part,
            tag_part.reshape(-1),
            loss_part[None],
        ]
    )
    n_small = small.shape[0]
    tail = small.astype(bf16)
    final = jnp.concatenate(
        [dx0.astype(bf16), as_rows(tail, cw)],
        axis=0,
    )
    final_all = lax.all_to_all(
        jnp.broadcast_to(final[None], (n_ctx,) + final.shape), "ctx", 0, 0, tiled=True
    )
    dx0_all = final_all[:, :rows].reshape(seq, cw).astype(f32)
    tail_all = final_all[:, rows:].reshape(n_ctx, -1).astype(f32)
    small_tot = jnp.sum(tail_all[:, :n_small], axis=0)
    n_dlog = rows * n_tags
    h_all = h_ids_all[:, :rows].reshape(seq, cw)
    extra = h_ids_all[:, rows:].reshape(n_ctx, -1)
    id_rows = extra[:, : 2 * rows].astype(jnp.int32)
    ids_all = (id_rows[:, :rows] * 32 + id_rows[:, rows : 2 * rows]).reshape(seq)
    dlog_rows = extra[:, 2 * rows : 2 * rows + 2 * n_dlog].astype(f32)
    dlog_all = (dlog_rows[:, :n_dlog] + dlog_rows[:, n_dlog:]).reshape(seq, n_tags)

    f_cols = width // n_ctx
    w_tag_cols = lax.dynamic_slice_in_dim(w_tag_full_t, k_ctx * f_cols, f_cols, 1)
    dy_all = jnp.dot(dlog_all, w_tag_cols, precision=high).astype(bf16)
    d_w_out = lax.dot_general(h_all, dy_all, (((0,), (0,)), ((), ())), preferred_element_type=f32)

    all_mask = ids_all[:, None] == vocab_ids[None, :]
    all_hot = all_mask.astype(bf16)
    r_all = jnp.sum(jnp.where(all_mask, r_vocab[None, :], 0.0), axis=1)[:, None]
    embed_k = lax.dynamic_slice_in_dim(embed_full, k_ctx * f_cols, f_cols, 1)
    gain_k = lax.dynamic_slice_in_dim(gain_full, k_ctx * f_cols, f_cols, 0)
    x0_k = jnp.dot(all_hot, embed_k, preferred_element_type=f32)
    u_k = (x0_k * r_all * gain_k[None, :]).astype(bf16)
    d_w_in = jnp.einsum("td,jtc->jdc", u_k, dp_all, preferred_element_type=f32)

    v_rows = vocab // n_ctx
    own_hot = (ids_all[:, None] == (k_ctx * v_rows + jnp.arange(v_rows))[None, :]).astype(f32)
    d_embed = jnp.dot(own_hot.T, dx0_all, precision=high)

    pos = 0
    outs = []
    for size, shape in (
        (cw, (cw,)),
        (3 * taps * cw, (3, taps, cw)),
        (span * cw, (span, cw)),
        (cw, (cw,)),
        (cw * n_tags, (cw, n_tags)),
        (1, ()),
    ):
        outs.append(small_tot[pos : pos + size].reshape(shape))
        pos += size
    gain_tot, short_tot, mr_tot, rate_tot, tag_tot, loss_tot = outs
    loss = loss_tot / seq
    return (
        loss,
        block_out,
        d_embed,
        gain_tot,
        d_w_in,
        short_tot,
        mr_tot,
        rate_tot,
        d_w_out,
        tag_tot,
    )


def solution(mesh):
    placed = (
        P("ctx"),
        P("ctx"),
        P(None, "dp"),
        P("dp"),
        P(None, None, "dp"),
        P(None, None, "dp"),
        P(None, "dp"),
        P("dp"),
        P("dp", None),
        P("dp", None),
    )
    return jax.shard_map(
        block,
        mesh=mesh,
        in_specs=placed,
        out_specs=(
            P(),
            P("ctx", "dp"),
            P("ctx", "dp"),
            P("dp"),
            P(None, "ctx", "dp"),
            P(None, None, "dp"),
            P(None, "dp"),
            P("dp"),
            P("dp", "ctx"),
            P("dp", None),
        ),
        check_vma=False,
    )
```

```python
import jax
import jax.numpy as jnp
from jax import lax
from jax.sharding import PartitionSpec as P
from jax.experimental import pallas as pl

LANES = 128
ROW_BLOCK = 64


def medium_forward(kv_ext, taps_eff, rows):
    span, width = taps_eff.shape

    def kernel(kv_ref, g_ref, m_ref):
        for rb in range(0, rows, ROW_BLOCK):

            def step(s, acc):
                start = span - 1 - s + rb
                return acc + g_ref[pl.ds(s, 1), :] * kv_ref[pl.ds(start, ROW_BLOCK), :]

            acc = lax.fori_loop(
                0, span, step, jnp.zeros((ROW_BLOCK, LANES), jnp.float32), unroll=8
            )
            m_ref[rb : rb + ROW_BLOCK, :] = acc

    ext = kv_ext.shape[0]
    return pl.pallas_call(
        kernel,
        out_shape=jax.ShapeDtypeStruct((rows, width), jnp.float32),
        grid=(width // LANES,),
        in_specs=[
            pl.BlockSpec((ext, LANES), lambda c: (0, c)),
            pl.BlockSpec((span, LANES), lambda c: (0, c)),
        ],
        out_specs=pl.BlockSpec((rows, LANES), lambda c: (0, c)),
    )(kv_ext, taps_eff)


def medium_backward(dm_ext, kv_ext, taps_eff, rows):
    span, width = taps_eff.shape

    def kernel(dm_ref, kv_ref, g_ref, dkv_ref, corr_ref):
        for rb in range(0, rows, ROW_BLOCK):

            def step(s, acc):
                return acc + g_ref[pl.ds(s, 1), :] * dm_ref[pl.ds(s + rb, ROW_BLOCK), :]

            acc = lax.fori_loop(
                0, span, step, jnp.zeros((ROW_BLOCK, LANES), jnp.float32), unroll=8
            )
            dkv_ref[rb : rb + ROW_BLOCK, :] = acc

        for s0 in range(0, span, 8):
            parts = []
            for s in range(s0, s0 + 8):
                start = span - 1 - s
                part = jnp.zeros((8, LANES), jnp.float32)
                for rb in range(0, rows, 8):
                    part = part + dm_ref[rb : rb + 8, :] * kv_ref[start + rb : start + rb + 8, :]
                parts.append(jnp.sum(part, axis=0, keepdims=True))
            corr_ref[s0 : s0 + 8, :] = jnp.concatenate(parts, axis=0)

    ext = kv_ext.shape[0]
    return pl.pallas_call(
        kernel,
        out_shape=(
            jax.ShapeDtypeStruct((rows, width), jnp.float32),
            jax.ShapeDtypeStruct((span, width), jnp.float32),
        ),
        grid=(width // LANES,),
        in_specs=[
            pl.BlockSpec((dm_ext.shape[0], LANES), lambda c: (0, c)),
            pl.BlockSpec((ext, LANES), lambda c: (0, c)),
            pl.BlockSpec((span, LANES), lambda c: (0, c)),
        ],
        out_specs=(
            pl.BlockSpec((rows, LANES), lambda c: (0, c)),
            pl.BlockSpec((span, LANES), lambda c: (0, c)),
        ),
    )(dm_ext, kv_ext, taps_eff)


def shifted(block, axis, distance):
    devices = range(lax.axis_size(axis))
    route = [(i - distance, i) for i in devices if i - distance in devices]
    return lax.ppermute(block, axis, route)


def short_filter(padded, filters, count):
    taps = filters.shape[1]
    total = jnp.zeros((count,) + padded.shape[1:], jnp.float32)
    for s in range(taps):
        total = total + filters[None, :, s, :] * padded[taps - 1 - s : taps - 1 - s + count].astype(
            jnp.float32
        )
    return total


def split3(x):
    parts = []
    rest = x
    for _ in range(3):
        part = lax.reduce_precision(rest, exponent_bits=8, mantissa_bits=7)
        parts.append(part)
        rest = rest - part
    return [p.astype(jnp.bfloat16) for p in parts]


def split2(x):
    hi = lax.reduce_precision(x, exponent_bits=8, mantissa_bits=7)
    return [hi.astype(jnp.bfloat16), (x - hi).astype(jnp.bfloat16)]


def as_rows(flat, width):
    pad = (-flat.shape[0]) % width
    return jnp.pad(flat, (0, pad)).reshape(-1, width)


def block(ids, tags, embed, gain, w_in, short_filt, mr_filt, rates, w_out, w_tag):
    f32 = jnp.float32
    bf16 = jnp.bfloat16
    high = lax.Precision.HIGHEST
    rows = ids.shape[0]
    vocab = embed.shape[0]
    cw = embed.shape[1]
    width = w_in.shape[1]
    taps = short_filt.shape[1]
    span = mr_filt.shape[0]
    n_tags = w_tag.shape[1]
    n_ctx = lax.axis_size("ctx")
    k_ctx = lax.axis_index("ctx")
    seq = rows * n_ctx

    n_dp = lax.axis_size("dp")
    half = vocab // 2
    packed = jnp.concatenate([embed[:half], jnp.stack(split3(gain), axis=0), w_tag.T], axis=0)
    packed_full = lax.all_gather(packed, "dp", axis=1, tiled=True)
    upper = lax.all_to_all(
        jnp.broadcast_to(embed[None, half:], (n_dp, vocab - half, cw)), "dp", 0, 0, tiled=True
    )
    upper_full = jnp.transpose(upper, (1, 0, 2)).reshape(vocab - half, width)
    w_out_later, upper_full = lax.optimization_barrier((w_out, upper_full))
    w_out_cols = lax.all_to_all(w_out_later, "dp", 1, 0, tiled=True)
    embed_full = jnp.concatenate([packed_full[:half], upper_full], axis=0)
    gain_full = (
        packed_full[half].astype(f32) + packed_full[half + 1].astype(f32)
    ) + packed_full[half + 2].astype(f32)
    w_tag_full_t = packed_full[half + 3 : half + 3 + n_tags].astype(f32)

    emb32 = embed_full.astype(f32)
    r_vocab = lax.rsqrt(jnp.sum(emb32 * emb32, axis=1) / width + 1e-06)
    vocab_ids = jnp.arange(vocab)
    id_mask = ids[:, None] == vocab_ids[None, :]
    id_hot = id_mask.astype(bf16)
    r = jnp.sum(jnp.where(id_mask, r_vocab[None, :], 0.0), axis=1)[:, None]
    x0_full = jnp.dot(id_hot, embed_full, preferred_element_type=f32)
    x0 = jnp.dot(id_hot, embed, preferred_element_type=f32)
    u = (x0_full * r * gain_full[None, :]).astype(bf16)
    proj = jnp.einsum("td,jdc->tjc", u, w_in, preferred_element_type=f32).astype(bf16)
    head = shifted(proj[rows - (taps - 1) :], "ctx", 1)
    p_ext = jnp.concatenate([head, proj], axis=0)
    z = short_filter(p_ext, short_filt, rows)
    kv = (z[:, 1] * z[:, 2]).astype(bf16)
    kv_head = shifted(kv[rows - (span - 1) :], "ctx", 1)
    kv_ext = jnp.concatenate([kv_head, kv, jnp.zeros((1,) + kv.shape[1:], kv.dtype)], axis=0)
    q = z[:, 0]
    k = z[:, 1]
    v = z[:, 2]
    lags = jnp.arange(span).astype(f32)[:, None]
    decay = jnp.exp(-rates[None, :] * lags)
    taps_eff = mr_filt * decay
    kv_wide = kv_ext.astype(f32)
    m = medium_forward(kv_wide, taps_eff, rows)
    h = (q * m).astype(bf16)
    h_full = lax.all_gather(h, "dp", axis=1, tiled=True)
    y = jnp.dot(h_full, w_out_cols, preferred_element_type=f32)
    block_out = (x0 + y).astype(bf16)
    id_hi = (ids // 32).astype(bf16)
    id_lo = (ids % 32).astype(bf16)
    logit_part = jnp.dot(block_out, w_tag, preferred_element_type=f32)
    logit_parts = lax.all_to_all(
        jnp.broadcast_to(logit_part[None], (n_dp,) + logit_part.shape), "dp", 0, 0, tiled=True
    )
    logits = jnp.sum(logit_parts, axis=0)
    top = jnp.max(logits, axis=1)
    lse = top + jnp.log(jnp.sum(jnp.exp(logits - top[:, None]), axis=1))
    tag_hot = (tags[:, None] == jnp.arange(n_tags)[None, :]).astype(f32)
    loss_part = jnp.sum(lse - jnp.sum(logits * tag_hot, axis=1))
    dlog = jnp.exp(logits - lse[:, None]) - tag_hot
    id_dlog = jnp.concatenate([id_hi, id_lo] + split2(dlog.reshape(-1)))
    h_ids = jnp.concatenate([h, as_rows(id_dlog, cw)], axis=0)
    h_ids_all = lax.all_to_all(
        jnp.broadcast_to(h_ids[None], (n_ctx,) + h_ids.shape), "ctx", 0, 0, tiled=True
    )
    dout = jnp.dot(dlog, w_tag.astype(f32).T, precision=high)
    tag_part = jnp.dot(block_out.astype(f32).T, dlog, precision=high)
    dy_full = jnp.dot(dlog, w_tag_full_t, precision=high).astype(bf16)
    dh = lax.dot_general(dy_full, w_out, (((1,), (1,)), ((), ())), preferred_element_type=f32)
    dq = dh * m
    dm = dh * q
    dm_tail = shifted(dm[: span - 1].astype(bf16), "ctx", -1).astype(f32)
    dm_ext = jnp.concatenate([dm, dm_tail, jnp.zeros((1,) + dm.shape[1:], f32)], axis=0)
    dkv, corr = medium_backward(dm_ext, kv_wide, taps_eff, rows)
    mr_part = corr * decay
    rate_part = -jnp.sum(lags * mr_filt * mr_part, axis=0)
    dz = jnp.stack([dq, dkv * v, dkv * k], axis=1)
    dz_tail = shifted(dz[: taps - 1], "ctx", -1)
    dz_ext = jnp.concatenate([dz, dz_tail], axis=0)
    dp = jnp.zeros_like(dz)
    shorts = []
    for s in range(taps):
        dp = dp + short_filt[None, :, s, :] * dz_ext[s : s + rows]
        shorts.append(jnp.sum(dz * p_ext[taps - 1 - s : taps - 1 - s + rows].astype(f32), axis=0))
    short_part = jnp.stack(shorts, axis=1)
    dpb = dp.astype(bf16)
    dp_all = lax.all_gather(jnp.transpose(dpb, (1, 0, 2)), "ctx", axis=1, tiled=True)
    du_part = jnp.einsum("tjc,jdc->td", dpb, w_in, preferred_element_type=f32)
    du_part, h_ids_all = lax.optimization_barrier((du_part, h_ids_all))
    dot_part = jnp.sum(du_part * gain_full[None, :] * x0_full, axis=1)
    dot_rows = as_rows(jnp.concatenate(split2(dot_part)), cw)
    n_dot = dot_rows.shape[0]
    du_send = jnp.concatenate(
        [
            du_part.astype(bf16).reshape(rows, n_dp, cw),
            jnp.broadcast_to(dot_rows[:, None, :], (n_dot, n_dp, cw)),
        ],
        axis=0,
    )
    du_recv = lax.all_to_all(du_send, "dp", 1, 1, tiled=True).astype(f32)
    du = jnp.sum(du_recv[:rows], axis=1)
    dot_recv = jnp.sum(du_recv[rows:], axis=1).reshape(-1)
    row_dot = (dot_recv[:rows] + dot_recv[rows : 2 * rows])[:, None] / width
    gain_part = jnp.sum(du * x0 * r, axis=0)
    dn = du * gain[None, :]
    dx0 = dout + r * (dn - x0 * r * r * row_dot)

    small = jnp.concatenate(
        [
            gain_part,
            short_part.reshape(-1),
            mr_part.reshape(-1),
            rate_part,
            tag_part.reshape(-1),
            loss_part[None],
        ]
    )
    n_small = small.shape[0]
    tail = small.astype(bf16)
    final = jnp.concatenate(
        [dx0.astype(bf16), as_rows(tail, cw)],
        axis=0,
    )
    final_all = lax.all_to_all(
        jnp.broadcast_to(final[None], (n_ctx,) + final.shape), "ctx", 0, 0, tiled=True
    )
    dx0_all = final_all[:, :rows].reshape(seq, cw).astype(f32)
    tail_all = final_all[:, rows:].reshape(n_ctx, -1).astype(f32)
    small_tot = jnp.sum(tail_all[:, :n_small], axis=0)
    n_dlog = rows * n_tags
    h_all = h_ids_all[:, :rows].reshape(seq, cw)
    extra = h_ids_all[:, rows:].reshape(n_ctx, -1)
    id_rows = extra[:, : 2 * rows].astype(jnp.int32)
    ids_all = (id_rows[:, :rows] * 32 + id_rows[:, rows : 2 * rows]).reshape(seq)
    dlog_rows = extra[:, 2 * rows : 2 * rows + 2 * n_dlog].astype(f32)
    dlog_all = (dlog_rows[:, :n_dlog] + dlog_rows[:, n_dlog:]).reshape(seq, n_tags)

    f_cols = width // n_ctx
    w_tag_cols = lax.dynamic_slice_in_dim(w_tag_full_t, k_ctx * f_cols, f_cols, 1)
    dy_all = jnp.dot(dlog_all, w_tag_cols, precision=high).astype(bf16)
    d_w_out = lax.dot_general(h_all, dy_all, (((0,), (0,)), ((), ())), preferred_element_type=f32)

    all_mask = ids_all[:, None] == vocab_ids[None, :]
    all_hot = all_mask.astype(bf16)
    r_all = jnp.sum(jnp.where(all_mask, r_vocab[None, :], 0.0), axis=1)[:, None]
    embed_k = lax.dynamic_slice_in_dim(embed_full, k_ctx * f_cols, f_cols, 1)
    gain_k = lax.dynamic_slice_in_dim(gain_full, k_ctx * f_cols, f_cols, 0)
    x0_k = jnp.dot(all_hot, embed_k, preferred_element_type=f32)
    u_k = (x0_k * r_all * gain_k[None, :]).astype(bf16)
    d_w_in = jnp.stack(
        [
            lax.dot_general(u_k, dp_all[j], (((0,), (0,)), ((), ())), preferred_element_type=f32)
            for j in range(dp_all.shape[0])
        ]
    )

    v_rows = vocab // n_ctx
    own_hot = (ids_all[:, None] == (k_ctx * v_rows + jnp.arange(v_rows))[None, :]).astype(f32)
    d_embed = jnp.dot(own_hot.T, dx0_all, precision=high)

    pos = 0
    outs = []
    for size, shape in (
        (cw, (cw,)),
        (3 * taps * cw, (3, taps, cw)),
        (span * cw, (span, cw)),
        (cw, (cw,)),
        (cw * n_tags, (cw, n_tags)),
        (1, ()),
    ):
        outs.append(small_tot[pos : pos + size].reshape(shape))
        pos += size
    gain_tot, short_tot, mr_tot, rate_tot, tag_tot, loss_tot = outs
    loss = loss_tot / seq
    return (
        loss,
        block_out,
        d_embed,
        gain_tot,
        d_w_in,
        short_tot,
        mr_tot,
        rate_tot,
        d_w_out,
        tag_tot,
    )


def solution(mesh):
    placed = (
        P("ctx"),
        P("ctx"),
        P(None, "dp"),
        P("dp"),
        P(None, None, "dp"),
        P(None, None, "dp"),
        P(None, "dp"),
        P("dp"),
        P("dp", None),
        P("dp", None),
    )
    return jax.shard_map(
        block,
        mesh=mesh,
        in_specs=placed,
        out_specs=(
            P(),
            P("ctx", "dp"),
            P("ctx", "dp"),
            P("dp"),
            P(None, "ctx", "dp"),
            P(None, None, "dp"),
            P(None, "dp"),
            P("dp"),
            P("dp", "ctx"),
            P("dp", None),
        ),
        check_vma=False,
    )
```
